256 devices in a mesh: ctx: 16 (over y, x), tp: 2 (over core), dp: 8 (over z).
Axes of the slice: x: 4, y: 4, z: 8, core: 2. Of those that a mesh axis runs over, the one named last changes fastest.
Arguments:
- nucleotides: int32 [65536], P(('dp', 'ctx')), parts along dimension 0, may hold values from 0 to 3
- complement: int32 [4], replicated, may hold values from 0 to 3, each once
- embedding: float32 [4, 1024], replicated, may hold values from -6 to 6
- w_gate: float32 [1024, 2048], P(None, 'tp'), may hold values from -0.1875 to 0.1875
- w_value: float32 [1024, 2048], P(None, 'tp'), may hold values from -0.1875 to 0.1875
- w_state: float32 [1024, 256], replicated, may hold values from -0.1875 to 0.1875
- w_step: float32 [1024, 32], P(None, 'tp'), may hold values from -0.1875 to 0.1875
- step_bias: float32 [32], P('tp'), may hold values from -5.5 to -4.5
- decay_rate: float32 [32], P('tp'), may hold values from 0 to 3
- conv_value: float32 [4, 2048], P(None, 'tp'), may hold values from -3 to 3
- conv_state: float32 [4, 256], replicated, may hold values from -3 to 3
- skip_gain: float32 [32], P('tp'), may hold values from 0.5 to 2
- norm_weight: float32 [2048], P('tp'), may hold values from 0.1 to 1.9
- w_out: float32 [2048, 1024], P('tp'), may hold values from -0.125 to 0.125
Outputs:
- mixed: float32 [65536, 1024], P(('dp', 'ctx', 'tp')), parts along dimension 0
The draws below stay inside these ranges and needn't reach their ends.
There are 8 independent parts, one for each index of `dp`. The reference program is written for one: setup_inputs(seed, part) draws one part's arguments, and reference() takes and returns one part's arrays. A program takes and returns all parts, laid end to end along the dimension named above; an argument that names none is the same for every part. Nothing has to cross between parts.
Inputs may be any that keep to these rules, and one draw needn't show every extreme that they name: `complement`: a permutation of the 4 nucleotide ids.
All inputs are finite; a program needn't handle non-finite values.
Results may differ from the reference program's by a relative error of at most 0.00023.
Values sent between devices are 32-bit elements; how exact they have to be, the bound alone decides.
No kernel may reach another device: no remote copies, remote signals or barrier semaphores. Data moves between devices by JAX's collectives and lax.ppermute only.
A program may use at most 128 MiB of HBM per device.

```python
import jax
import jax.numpy as jnp
from jax import lax

D = 1024
HEADS = 32
HEAD_DIM = 64
INNER = 2048
STATE = 128
VOCAB = 4
CONV = 4
BLK = 256
TOKENS = 8192


def draw_decay_rate(key, part):
    lowest = 20.0 / TOKENS
    uniform_draw = jax.random.uniform(key, (HEADS,), jnp.float32, 0.0, 1.0)
    result = lowest * jnp.exp(uniform_draw * jnp.log(3.0 / lowest))
    return result


def set_ends(values, key, smallest, top_value):
    longest = values.shape.index(max(values.shape))
    spots = []
    for shift in (0, 1):
        where = [jax.random.randint(jax.random.fold_in(key, axis), (), 0, length) for axis, length in enumerate(values.shape)]
        where[longest] = (where[longest] + shift) % values.shape[longest]
        spots.append(tuple(where))
    return values.at[spots[0]].set(smallest).at[spots[1]].set(top_value)


def shard_levels(key, extent, shards, smallest, top_value):
    factor_of = 1.0
    for axis_at, blocks in shards:
        steps = jax.random.uniform(jax.random.fold_in(jax.random.fold_in(key, 6), axis_at), (blocks,), jnp.float32, smallest / len(shards), top_value / len(shards))
        factor_of = factor_of * jnp.repeat(jnp.exp(steps), extent[axis_at] // blocks).reshape((-1,) + (1,) * (len(extent) - 1 - axis_at))
    return factor_of


def noise(stream_key, dims, width, reach, shards=(), kind=jnp.bfloat16):
    drawn = jax.random.normal(stream_key, dims, jnp.float32) * width
    if len(shards) > 0:
        drawn = shard_levels(stream_key, dims, shards, -0.22, 0.18) * drawn
    return jnp.clip(drawn, min=-reach, max=reach).astype(kind)


def setup_inputs(seed: int = 0, part: int = 0) -> dict:
    streams_of = jax.random.split(jax.random.key(seed), 15)
    own_keys = jax.random.split(jax.random.fold_in(streams_of[14], part), 15)
    return {
        "nucleotides": set_ends(jax.random.randint(own_keys[0], (TOKENS,), 0, VOCAB), jax.random.fold_in(own_keys[0], 1), 0, VOCAB - 1).astype(jnp.int32),
        "complement": jax.random.permutation(streams_of[1], VOCAB).astype(jnp.int32),
        "embedding": noise(streams_of[2], (VOCAB, D), 1.0, 6.0, (), jnp.float32),
        "w_gate": noise(streams_of[3], (D, INNER), D ** -0.5, 0.1875, ((1, 2),), jnp.float32),
        "w_value": noise(streams_of[4], (D, INNER), D ** -0.5, 0.1875, ((1, 2),), jnp.float32),
        "w_state": noise(streams_of[5], (D, 2 * STATE), D ** -0.5, 0.1875, (), jnp.float32),
        "w_step": noise(streams_of[6], (D, HEADS), D ** -0.5, 0.1875, ((1, 2),), jnp.float32),
        "step_bias": jnp.clip(-5.5 + 1.0 * jax.random.uniform(streams_of[7], (HEADS,), jnp.float32) ** shard_levels(streams_of[7], (HEADS,), ((0, 2),), -0.2, 0.2), -5.5, -4.5),
        "decay_rate": draw_decay_rate(jax.random.fold_in(streams_of[14], 71), part),
        "conv_value": noise(streams_of[9], (CONV, INNER), CONV ** -0.5, 3.0, ((1, 2),), jnp.float32),
        "conv_state": noise(streams_of[10], (CONV, 2 * STATE), CONV ** -0.5, 3.0, (), jnp.float32),
        "skip_gain": jnp.clip(0.5 + 1.5 * jax.random.uniform(streams_of[11], (HEADS,), jnp.float32) ** shard_levels(streams_of[11], (HEADS,), ((0, 2),), -0.2, 0.2), 0.5, 2.0),
        "norm_weight": jnp.clip(1.0 + 0.18 * jax.random.normal(streams_of[12], (INNER,), jnp.float32), 0.1, 1.9),
        "w_out": noise(streams_of[13], (INNER, D), INNER ** -0.5, 0.125, ((0, 2),), jnp.float32),
    }


HIGHEST = lax.Precision.HIGHEST
EPSILON = 1e-05

def causal_conv(padded, kernel):
    length = padded.shape[0] - kernel.shape[0] + 1
    output = jnp.zeros((length, padded.shape[1]), jnp.float32)
    for offset in range(kernel.shape[0]):
        output = output + kernel[offset][None, :] * padded[offset:offset + length]
    return output

def full_scan(values, b_in, c_out, log_step, step_size):
    length = values.shape[0]
    block_count = length // BLK
    block_data = (values.reshape(block_count, BLK, HEADS, HEAD_DIM), b_in.reshape(block_count, BLK, STATE), c_out.reshape(block_count, BLK, STATE), log_step.reshape(block_count, BLK, HEADS), step_size.reshape(block_count, BLK, HEADS))
    causal_mask = jnp.arange(BLK)[:, None] >= jnp.arange(BLK)[None, :]

    def advance(memory, block_items):
        block_values, block_b, block_c, block_log, block_step = block_items
        running = jnp.cumsum(block_log, axis=0)
        spread = jnp.where(causal_mask[:, :, None], running[:, None, :] - running[None, :, :], 0.0)
        weights = jnp.where(causal_mask[:, :, None], jnp.exp(spread), 0.0)
        intersection = jnp.dot(block_c, block_b.T, precision=HIGHEST)
        mixing = intersection[:, :, None] * weights * block_step[None, :, :]
        inside = jnp.einsum('ijh,jhp->ihp', mixing, block_values, precision=HIGHEST)
        carried = jnp.einsum('in,hpn->ihp', block_c, memory, precision=HIGHEST) * jnp.exp(running)[:, :, None]
        weighting = jnp.exp(running[-1][None, :] - running) * block_step
        memory = memory * jnp.exp(running[-1])[:, None, None] + jnp.einsum('jh,jhp,jn->hpn', weighting, block_values, block_b, precision=HIGHEST)
        return (memory, inside + carried)
    initial = jnp.zeros((HEADS, HEAD_DIM, STATE), jnp.float32)
    memory, outputs = lax.scan(advance, initial, block_data)
    return outputs.reshape(length, HEADS, HEAD_DIM)

def strand(sequence, embedding, w_gate, w_value, w_state, w_step, step_bias, decay_rate, conv_value, conv_state, skip_gain, norm_weight):
    table = jnp.concatenate([w_gate, w_value, w_state, w_step], axis=1)
    projected = jnp.dot(embedding, table, precision=HIGHEST)
    rows_in = projected[sequence]
    gate = rows_in[:, :INNER]
    value_raw = rows_in[:, INNER:2 * INNER]
    state_raw = rows_in[:, 2 * INNER:2 * INNER + 2 * STATE]
    step_size = jax.nn.softplus(rows_in[:, 2 * INNER + 2 * STATE:] + step_bias[None, :])
    value_pad = jnp.zeros((CONV - 1, INNER), jnp.float32)
    state_pad = jnp.zeros((CONV - 1, 2 * STATE), jnp.float32)
    values = jax.nn.silu(causal_conv(jnp.concatenate([value_pad, value_raw], axis=0), conv_value))
    maps = jax.nn.silu(causal_conv(jnp.concatenate([state_pad, state_raw], axis=0), conv_state))
    b_in = maps[:, :STATE]
    c_out = maps[:, STATE:]
    head_values = values.reshape(-1, HEADS, HEAD_DIM)
    outputs = full_scan(head_values, b_in, c_out, -decay_rate[None, :] * step_size, step_size)
    outputs = outputs + skip_gain[None, :, None] * head_values
    gated = outputs.reshape(-1, INNER) * jax.nn.silu(gate)
    scale = lax.rsqrt(lax.optimization_barrier(jnp.mean(gated * gated, axis=1, keepdims=True)) + EPSILON)
    return gated * scale * norm_weight[None, :]

def reference(nucleotides, complement, embedding, w_gate, w_value, w_state, w_step, step_bias, decay_rate, conv_value, conv_state, skip_gain, norm_weight, w_out):
    forward_normed = strand(nucleotides, embedding, w_gate, w_value, w_state, w_step, step_bias, decay_rate, conv_value, conv_state, skip_gain, norm_weight)
    reverse_ids = complement[nucleotides][::-1]
    reverse_normed = strand(reverse_ids, embedding, w_gate, w_value, w_state, w_step, step_bias, decay_rate, conv_value, conv_state, skip_gain, norm_weight)
    return jnp.dot(forward_normed + reverse_normed[::-1], w_out, precision=HIGHEST)
```

```python
import jax
import jax.numpy as jnp
from jax import lax
from jax.sharding import PartitionSpec as P

CONV = 4
BLK = 256


HIGHEST = lax.Precision.HIGHEST
EPSILON = 1e-05


def shifted(value, axis, steps):
    count = lax.axis_size(axis)
    first, last = (max(0, -steps), min(count, count - steps))
    return lax.ppermute(value, axis, [(source, source + steps) for source in range(first, last)])


def causal_conv(padded, kernel):
    length = padded.shape[0] - kernel.shape[0] + 1
    output = jnp.zeros((length, padded.shape[1]), jnp.float32)
    for offset in range(kernel.shape[0]):
        output = output + kernel[offset][None, :] * padded[offset : offset + length]
    return output


def strand_local(joined_in, rim_rows, kernel, step_raw, step_bias, decay_rate, inner_local,
                 state_size, head_dim, block_rows):
    convolved = jax.nn.silu(causal_conv(jnp.concatenate([rim_rows, joined_in], axis=0), kernel))
    length = joined_in.shape[0]
    head_count = inner_local // head_dim
    block_count = length // block_rows
    values = convolved[:, :inner_local]
    b_in = convolved[:, inner_local : inner_local + state_size]
    c_out = convolved[:, inner_local + state_size :]
    step_size = jax.nn.softplus(step_raw + step_bias[None, :])
    log_step = -decay_rate[None, :] * step_size

    xs = values.reshape(block_count, block_rows, head_count, head_dim).transpose(0, 2, 1, 3)
    bs = b_in.reshape(block_count, block_rows, state_size)
    cs = c_out.reshape(block_count, block_rows, state_size)
    logs = log_step.reshape(block_count, block_rows, head_count).transpose(0, 2, 1)
    steps = step_size.reshape(block_count, block_rows, head_count).transpose(0, 2, 1)
    running = jnp.cumsum(logs, axis=2)
    totals = running[:, :, -1]

    weighting = jnp.exp(totals[:, :, None] - running) * steps
    ends = jnp.einsum("bhj,bhjp,bjn->bhpn", weighting, xs, bs, precision=HIGHEST)
    prefix = [jnp.zeros_like(ends[0])]
    for block in range(1, block_count):
        prefix.append(jnp.exp(totals[block - 1])[:, None, None] * prefix[-1] + ends[block - 1])
    memory = jnp.exp(totals[-1])[:, None, None] * prefix[-1] + ends[-1]
    prefix = jnp.stack(prefix)
    offsets = jnp.cumsum(totals, axis=0) - totals
    total_log = jnp.sum(totals, axis=0)

    causal = (jnp.arange(block_rows)[:, None] >= jnp.arange(block_rows)[None, :])[None, None]
    spread = jnp.where(causal, running[:, :, :, None] - running[:, :, None, :], 0.0)
    weights = jnp.where(causal, jnp.exp(spread), 0.0)
    intersection = jnp.einsum("bin,bjn->bij", cs, bs, precision=HIGHEST)
    mixing = intersection[:, None] * weights * steps[:, :, None, :]
    inside = jnp.einsum("bhij,bhjp->bhip", mixing, xs, precision=HIGHEST)
    return dict(xs=xs, cs=cs, running=running, prefix=prefix, offsets=offsets, memory=memory,
                total_log=total_log, inside=inside)


def finish_strand(parts, incoming, skip_gain, gate):
    entering = jnp.exp(parts["offsets"])[:, :, None, None] * incoming[None] + parts["prefix"]
    carried = jnp.einsum("bin,bhpn->bhip", parts["cs"], entering, precision=HIGHEST)
    outputs = parts["inside"] + carried * jnp.exp(parts["running"])[..., None]
    outputs = outputs + skip_gain[None, :, None, None] * parts["xs"]
    outputs = outputs.transpose(0, 2, 1, 3).reshape(gate.shape)
    return outputs * jax.nn.silu(gate)


def relay(total_log, memory, axis, direction):
    count = lax.axis_size(axis)
    factor = shifted(jnp.exp(total_log), axis, direction)
    state = shifted(memory, axis, direction)
    distance = 1
    while distance < count:
        factor_in = shifted(factor, axis, direction * distance)
        state_in = shifted(state, axis, direction * distance)
        state = state + factor[:, None, None] * state_in
        factor = factor * factor_in
        distance *= 2
    return state


def local(
    nucleotides,
    complement,
    embedding,
    w_gate,
    w_value,
    w_state,
    w_step,
    step_bias,
    decay_rate,
    conv_value,
    conv_state,
    skip_gain,
    norm_weight,
    w_out,
):
    inner_local = w_gate.shape[1]
    state_size = w_state.shape[1] // 2
    head_count = step_bias.shape[0]
    head_dim = inner_local // head_count
    vocab_size = embedding.shape[0]
    table = jnp.concatenate([w_gate, w_value, w_state, w_step], axis=1)
    projected = jnp.dot(embedding, table, precision=HIGHEST)
    kernel = jnp.concatenate([conv_value, conv_state], axis=1)
    symbols = jnp.arange(vocab_size, dtype=jnp.int32)
    forward_match = nucleotides[:, None] == symbols[None, :]
    paired_ids = jnp.sum(jnp.where(forward_match, complement[None, :], 0), axis=1)
    reverse_hot = (paired_ids[::-1][:, None] == symbols[None, :]).astype(jnp.float32)
    forward_hot = forward_match.astype(jnp.float32)
    edge_rows = CONV - 1
    rim_forward_hot = shifted(forward_hot[-edge_rows:], "ctx", 1)
    rim_reverse_hot = shifted(reverse_hot[-edge_rows:], "ctx", -1)
    split_step = 2 * inner_local + 2 * state_size
    conv_table = projected[:, inner_local:split_step]
    forward_rows = jnp.dot(forward_hot, projected, precision=HIGHEST)
    reverse_rows = jnp.dot(reverse_hot, projected, precision=HIGHEST)
    rim_forward = jnp.dot(rim_forward_hot, conv_table, precision=HIGHEST)
    rim_reverse = jnp.dot(rim_reverse_hot, conv_table, precision=HIGHEST)
    parts_f = strand_local(forward_rows[:, inner_local:split_step], rim_forward, kernel,
                           forward_rows[:, split_step:], step_bias, decay_rate, inner_local,
                           state_size, head_dim, BLK)
    parts_r = strand_local(reverse_rows[:, inner_local:split_step], rim_reverse, kernel,
                           reverse_rows[:, split_step:], step_bias, decay_rate, inner_local,
                           state_size, head_dim, BLK)
    incoming_f = relay(parts_f["total_log"], parts_f["memory"], "ctx", 1)
    incoming_r = relay(parts_r["total_log"], parts_r["memory"], "ctx", -1)
    gated_f = finish_strand(parts_f, incoming_f, skip_gain, forward_rows[:, :inner_local])
    gated_r = finish_strand(parts_r, incoming_r, skip_gain, reverse_rows[:, :inner_local])
    square_sums = lax.psum(
        (jnp.sum(gated_f * gated_f, axis=1), jnp.sum(gated_r * gated_r, axis=1)), "tp"
    )
    width_all = inner_local * lax.axis_size("tp")
    normed_f = (
        gated_f * lax.rsqrt(square_sums[0] / width_all + EPSILON)[:, None] * norm_weight[None, :]
    )
    normed_r = (
        gated_r * lax.rsqrt(square_sums[1] / width_all + EPSILON)[:, None] * norm_weight[None, :]
    )
    combined = normed_f + normed_r[::-1]
    partial = jnp.dot(combined, w_out, precision=HIGHEST)
    return lax.psum_scatter(partial, "tp", scatter_dimension=0, tiled=True)


def solution(mesh):
    placed = (
        P(("dp", "ctx")),
        P(),
        P(),
        P(None, "tp"),
        P(None, "tp"),
        P(),
        P(None, "tp"),
        P("tp"),
        P("tp"),
        P(None, "tp"),
        P(),
        P("tp"),
        P("tp"),
        P("tp", None),
    )
    return jax.shard_map(
        local, mesh=mesh, in_specs=placed, out_specs=P(("dp", "ctx", "tp"), None), check_vma=False
    )
```

```python
import jax
import jax.numpy as jnp
from jax import lax
from jax.sharding import PartitionSpec as P

CONV = 4
BLK = 256


HIGHEST = lax.Precision.HIGHEST
EPSILON = 1e-05


def shifted(value, axis, steps):
    count = lax.axis_size(axis)
    first, last = (max(0, -steps), min(count, count - steps))
    return lax.ppermute(value, axis, [(source, source + steps) for source in range(first, last)])


def causal_conv(padded, kernel):
    length = padded.shape[0] - kernel.shape[0] + 1
    output = jnp.zeros((length, padded.shape[1]), jnp.float32)
    for offset in range(kernel.shape[0]):
        output = output + kernel[offset][None, :] * padded[offset : offset + length]
    return output


def strand_local(joined_in, rim_rows, kernel, step_raw, step_bias, decay_rate, skip_gain,
                 gate, inner_local, state_size, head_dim, block_rows, backward):
    if backward:
        padded = jnp.concatenate([joined_in, rim_rows], axis=0)
        kernel = kernel[::-1]
    else:
        padded = jnp.concatenate([rim_rows, joined_in], axis=0)
    convolved = jax.nn.silu(causal_conv(padded, kernel))
    length = joined_in.shape[0]
    head_count = inner_local // head_dim
    block_count = length // block_rows
    values = convolved[:, :inner_local]
    b_in = convolved[:, inner_local : inner_local + state_size]
    c_out = convolved[:, inner_local + state_size :]
    step_size = jax.nn.softplus(step_raw + step_bias[None, :])
    log_step = -decay_rate[None, :] * step_size

    xs = values.reshape(block_count, block_rows, head_count, head_dim).transpose(0, 2, 1, 3)
    bs = b_in.reshape(block_count, block_rows, state_size)
    cs = c_out.reshape(block_count, block_rows, state_size)
    logs = log_step.reshape(block_count, block_rows, head_count).transpose(0, 2, 1)
    steps = step_size.reshape(block_count, block_rows, head_count).transpose(0, 2, 1)
    running = lax.cumsum(logs, axis=2, reverse=backward)
    totals = running[:, :, 0] if backward else running[:, :, -1]

    weighting = jnp.exp(totals[:, :, None] - running) * steps
    ends = jnp.einsum("bhj,bhjp,bjn->bhpn", weighting, xs, bs, precision=HIGHEST)
    order = list(range(block_count))
    if backward:
        order = order[::-1]
    prefix = {order[0]: jnp.zeros_like(ends[0])}
    for before, block in zip(order[:-1], order[1:]):
        prefix[block] = jnp.exp(totals[before])[:, None, None] * prefix[before] + ends[before]
    last = order[-1]
    memory = jnp.exp(totals[last])[:, None, None] * prefix[last] + ends[last]
    prefix = jnp.stack([prefix[block] for block in range(block_count)])
    offsets = lax.cumsum(totals, axis=0, reverse=backward) - totals
    total_log = jnp.sum(totals, axis=0)

    rows = jnp.arange(block_rows)[:, None]
    cols = jnp.arange(block_rows)[None, :]
    causal = ((rows <= cols) if backward else (rows >= cols))[None, None]
    spread = jnp.where(causal, running[:, :, :, None] - running[:, :, None, :], 0.0)
    weights = jnp.where(causal, jnp.exp(spread), 0.0)
    intersection = jnp.einsum("bin,bjn->bij", cs, bs, precision=HIGHEST)
    mixing = intersection[:, None] * weights * steps[:, :, None, :]
    inside = jnp.einsum("bhij,bhjp->bhip", mixing, xs, precision=HIGHEST)
    carried = jnp.einsum("bin,bhpn->bhip", cs, prefix, precision=HIGHEST)
    outputs = inside + carried * jnp.exp(running)[..., None]
    outputs = outputs + skip_gain[None, :, None, None] * xs
    outputs = outputs.transpose(0, 2, 1, 3).reshape(length, inner_local)
    reach = (offsets[:, :, None] + running).transpose(0, 2, 1).reshape(length, head_count)
    return dict(outputs=outputs, c_out=c_out, reach=reach, memory=memory, total_log=total_log,
                gate=jax.nn.silu(gate))


def finish_strand(parts, incoming):
    entering = jnp.einsum("tn,hpn->thp", parts["c_out"], incoming, precision=HIGHEST)
    entering = entering * jnp.exp(parts["reach"])[:, :, None]
    outputs = parts["outputs"] + entering.reshape(parts["outputs"].shape)
    return outputs * parts["gate"]


def relay(total_log, memory, axis, direction):
    count = lax.axis_size(axis)
    factor = shifted(jnp.exp(total_log), axis, direction)
    state = shifted(memory, axis, direction)
    distance = 1
    while distance < count:
        factor_in = shifted(factor, axis, direction * distance)
        state_in = shifted(state, axis, direction * distance)
        state = state + factor[:, None, None] * state_in
        factor = factor * factor_in
        distance *= 2
    return state


def local(
    nucleotides,
    complement,
    embedding,
    w_gate,
    w_value,
    w_state,
    w_step,
    step_bias,
    decay_rate,
    conv_value,
    conv_state,
    skip_gain,
    norm_weight,
    w_out,
):
    inner_local = w_gate.shape[1]
    state_size = w_state.shape[1] // 2
    head_count = step_bias.shape[0]
    head_dim = inner_local // head_count
    vocab_size = embedding.shape[0]
    table = jnp.concatenate([w_gate, w_value, w_state, w_step], axis=1)
    projected = jnp.dot(embedding, table, precision=HIGHEST)
    kernel = jnp.concatenate([conv_value, conv_state], axis=1)
    symbols = jnp.arange(vocab_size, dtype=jnp.int32)
    forward_match = nucleotides[:, None] == symbols[None, :]
    paired_ids = jnp.sum(jnp.where(forward_match, complement[None, :], 0), axis=1)
    reverse_hot = (paired_ids[:, None] == symbols[None, :]).astype(jnp.float32)
    forward_hot = forward_match.astype(jnp.float32)
    edge_rows = CONV - 1
    rim_forward_hot = shifted(forward_hot[-edge_rows:], "ctx", 1)
    rim_reverse_hot = shifted(reverse_hot[:edge_rows], "ctx", -1)
    split_step = 2 * inner_local + 2 * state_size
    conv_table = projected[:, inner_local:split_step]
    forward_rows = jnp.dot(forward_hot, projected, precision=HIGHEST)
    reverse_rows = jnp.dot(reverse_hot, projected, precision=HIGHEST)
    rim_forward = jnp.dot(rim_forward_hot, conv_table, precision=HIGHEST)
    rim_reverse = jnp.dot(rim_reverse_hot, conv_table, precision=HIGHEST)
    parts_f = strand_local(forward_rows[:, inner_local:split_step], rim_forward, kernel,
                           forward_rows[:, split_step:], step_bias, decay_rate, skip_gain,
                           forward_rows[:, :inner_local], inner_local, state_size, head_dim, BLK,
                           False)
    parts_r = strand_local(reverse_rows[:, inner_local:split_step], rim_reverse, kernel,
                           reverse_rows[:, split_step:], step_bias, decay_rate, skip_gain,
                           reverse_rows[:, :inner_local], inner_local, state_size, head_dim, BLK,
                           True)
    incoming_f = relay(parts_f["total_log"], parts_f["memory"], "ctx", 1)
    incoming_r = relay(parts_r["total_log"], parts_r["memory"], "ctx", -1)
    gated_f = finish_strand(parts_f, incoming_f)
    gated_r = finish_strand(parts_r, incoming_r)
    square_sums = lax.psum(
        (jnp.sum(gated_f * gated_f, axis=1), jnp.sum(gated_r * gated_r, axis=1)), "tp"
    )
    width_all = inner_local * lax.axis_size("tp")
    normed_f = (
        gated_f * lax.rsqrt(square_sums[0] / width_all + EPSILON)[:, None] * norm_weight[None, :]
    )
    normed_r = (
        gated_r * lax.rsqrt(square_sums[1] / width_all + EPSILON)[:, None] * norm_weight[None, :]
    )
    combined = normed_f + normed_r
    partial = jnp.dot(combined, w_out, precision=HIGHEST)
    return lax.psum_scatter(partial, "tp", scatter_dimension=0, tiled=True)


def solution(mesh):
    placed = (
        P(("dp", "ctx")),
        P(),
        P(),
        P(None, "tp"),
        P(None, "tp"),
        P(),
        P(None, "tp"),
        P("tp"),
        P("tp"),
        P(None, "tp"),
        P(),
        P("tp"),
        P("tp"),
        P("tp", None),
    )
    return jax.shard_map(
        local, mesh=mesh, in_specs=placed, out_specs=P(("dp", "ctx", "tp"), None), check_vma=False
    )
```

```python
import jax
import jax.numpy as jnp
from jax import lax
from jax.sharding import PartitionSpec as P

CONV = 4
BLK = 256


HIGHEST = lax.Precision.HIGHEST
EPSILON = 1e-05


def shifted(value, axis, steps):
    count = lax.axis_size(axis)
    first, last = (max(0, -steps), min(count, count - steps))
    return lax.ppermute(value, axis, [(source, source + steps) for source in range(first, last)])


def causal_conv(padded, kernel):
    length = padded.shape[0] - kernel.shape[0] + 1
    output = jnp.zeros((length, padded.shape[1]), jnp.float32)
    for offset in range(kernel.shape[0]):
        output = output + kernel[offset][None, :] * padded[offset : offset + length]
    return output


def strand_local(joined_in, rim_rows, kernel, step_raw, step_bias, decay_rate, skip_gain,
                 gate, inner_local, state_size, head_dim, block_rows, backward):
    if backward:
        padded = jnp.concatenate([joined_in, rim_rows], axis=0)
        kernel = kernel[::-1]
    else:
        padded = jnp.concatenate([rim_rows, joined_in], axis=0)
    convolved = jax.nn.silu(causal_conv(padded, kernel))
    length = joined_in.shape[0]
    head_count = inner_local // head_dim
    block_count = length // block_rows
    values = convolved[:, :inner_local]
    b_in = convolved[:, inner_local : inner_local + state_size]
    c_out = convolved[:, inner_local + state_size :]
    step_size = jax.nn.softplus(step_raw + step_bias[None, :])
    log_step = -decay_rate[None, :] * step_size

    xs = values.reshape(block_count, block_rows, head_count, head_dim).transpose(0, 2, 1, 3)
    bs = b_in.reshape(block_count, block_rows, state_size)
    cs = c_out.reshape(block_count, block_rows, state_size)
    logs = log_step.reshape(block_count, block_rows, head_count).transpose(0, 2, 1)
    steps = step_size.reshape(block_count, block_rows, head_count).transpose(0, 2, 1)
    running = lax.cumsum(logs, axis=2, reverse=backward)
    totals = running[:, :, 0] if backward else running[:, :, -1]

    weighting = jnp.exp(totals[:, :, None] - running) * steps
    ends = jnp.einsum("bhj,bhjp,bjn->bhpn", weighting, xs, bs, precision=HIGHEST)
    order = list(range(block_count))
    if backward:
        order = order[::-1]
    prefix = {order[0]: jnp.zeros_like(ends[0])}
    for before, block in zip(order[:-1], order[1:]):
        prefix[block] = jnp.exp(totals[before])[:, None, None] * prefix[before] + ends[before]
    last = order[-1]
    memory = jnp.exp(totals[last])[:, None, None] * prefix[last] + ends[last]
    prefix = jnp.stack([prefix[block] for block in range(block_count)])
    offsets = lax.cumsum(totals, axis=0, reverse=backward) - totals
    total_log = jnp.sum(totals, axis=0)

    rows = jnp.arange(block_rows)[:, None]
    cols = jnp.arange(block_rows)[None, :]
    causal = ((rows <= cols) if backward else (rows >= cols))[None, None]
    spread = jnp.where(causal, running[:, :, :, None] - running[:, :, None, :], 0.0)
    weights = jnp.where(causal, jnp.exp(spread), 0.0)
    intersection = jnp.einsum("bin,bjn->bij", cs, bs, precision=HIGHEST)
    mixing = intersection[:, None] * weights * steps[:, :, None, :]
    inside = jnp.einsum("bhij,bhjp->bhip", mixing, xs, precision=HIGHEST)
    carried = jnp.einsum("bin,bhpn->bhip", cs, prefix, precision=HIGHEST)
    outputs = inside + carried * jnp.exp(running)[..., None]
    outputs = outputs + skip_gain[None, :, None, None] * xs
    outputs = outputs.transpose(0, 2, 1, 3).reshape(length, inner_local)
    reach = (offsets[:, :, None] + running).transpose(0, 2, 1).reshape(length, head_count)
    return dict(outputs=outputs, c_out=c_out, reach=reach, memory=memory, total_log=total_log,
                gate=jax.nn.silu(gate))


def finish_strand(parts, incoming):
    entering = jnp.einsum("tn,hpn->thp", parts["c_out"], incoming, precision=HIGHEST)
    entering = entering * jnp.exp(parts["reach"])[:, :, None]
    outputs = parts["outputs"] + entering.reshape(parts["outputs"].shape)
    return outputs * parts["gate"]


def relay(total_log, memory, axis, direction):
    count = lax.axis_size(axis)
    head_count, head_dim, state_size = memory.shape
    factor = jnp.broadcast_to(jnp.exp(total_log)[:, None, None], (head_count, 1, state_size))
    packed = shifted(jnp.concatenate([memory, factor], axis=1), axis, direction)
    distance = 1
    while distance < count:
        arrived = shifted(packed, axis, direction * distance)
        state = packed[:, :head_dim] + packed[:, head_dim:] * arrived[:, :head_dim]
        factor = packed[:, head_dim:] * arrived[:, head_dim:]
        packed = jnp.concatenate([state, factor], axis=1)
        distance *= 2
    return packed[:, :head_dim]


def local(
    nucleotides,
    complement,
    embedding,
    w_gate,
    w_value,
    w_state,
    w_step,
    step_bias,
    decay_rate,
    conv_value,
    conv_state,
    skip_gain,
    norm_weight,
    w_out,
):
    inner_local = w_gate.shape[1]
    state_size = w_state.shape[1] // 2
    head_count = step_bias.shape[0]
    head_dim = inner_local // head_count
    vocab_size = embedding.shape[0]
    table = jnp.concatenate([w_gate, w_value, w_state, w_step], axis=1)
    projected = jnp.dot(embedding, table, precision=HIGHEST)
    kernel = jnp.concatenate([conv_value, conv_state], axis=1)
    symbols = jnp.arange(vocab_size, dtype=jnp.int32)
    forward_match = nucleotides[:, None] == symbols[None, :]
    paired_ids = jnp.sum(jnp.where(forward_match, complement[None, :], 0), axis=1)
    reverse_hot = (paired_ids[:, None] == symbols[None, :]).astype(jnp.float32)
    forward_hot = forward_match.astype(jnp.float32)
    edge_rows = CONV - 1
    rim_forward_hot = shifted(forward_hot[-edge_rows:], "ctx", 1)
    rim_reverse_hot = shifted(reverse_hot[:edge_rows], "ctx", -1)
    split_step = 2 * inner_local + 2 * state_size
    conv_table = projected[:, inner_local:split_step]
    forward_rows = jnp.dot(forward_hot, projected, precision=HIGHEST)
    reverse_rows = jnp.dot(reverse_hot, projected, precision=HIGHEST)
    rim_forward = jnp.dot(rim_forward_hot, conv_table, precision=HIGHEST)
    rim_reverse = jnp.dot(rim_reverse_hot, conv_table, precision=HIGHEST)
    parts_f = strand_local(forward_rows[:, inner_local:split_step], rim_forward, kernel,
                           forward_rows[:, split_step:], step_bias, decay_rate, skip_gain,
                           forward_rows[:, :inner_local], inner_local, state_size, head_dim, BLK,
                           False)
    parts_r = strand_local(reverse_rows[:, inner_local:split_step], rim_reverse, kernel,
                           reverse_rows[:, split_step:], step_bias, decay_rate, skip_gain,
                           reverse_rows[:, :inner_local], inner_local, state_size, head_dim, BLK,
                           True)
    incoming_f = relay(parts_f["total_log"], parts_f["memory"], "ctx", 1)
    incoming_r = relay(parts_r["total_log"], parts_r["memory"], "ctx", -1)
    gated_f = finish_strand(parts_f, incoming_f)
    gated_r = finish_strand(parts_r, incoming_r)
    square_sums = lax.psum(
        (jnp.sum(gated_f * gated_f, axis=1), jnp.sum(gated_r * gated_r, axis=1)), "tp"
    )
    width_all = inner_local * lax.axis_size("tp")
    normed_f = (
        gated_f * lax.rsqrt(square_sums[0] / width_all + EPSILON)[:, None] * norm_weight[None, :]
    )
    normed_r = (
        gated_r * lax.rsqrt(square_sums[1] / width_all + EPSILON)[:, None] * norm_weight[None, :]
    )
    combined = normed_f + normed_r
    tp_count = lax.axis_size("tp")
    rows_each = combined.shape[0] // tp_count
    own = lax.axis_index("tp")
    result = None
    for turn in range(1, tp_count):
        target = (own + turn) % tp_count
        rows = lax.dynamic_slice_in_dim(combined, target * rows_each, rows_each, 0)
        partial = jnp.dot(rows, w_out, precision=HIGHEST)
        pairs = [(source, (source + turn) % tp_count) for source in range(tp_count)]
        arrived = lax.ppermute(partial, "tp", pairs)
        result = arrived if result is None else result + arrived
    rows = lax.dynamic_slice_in_dim(combined, own * rows_each, rows_each, 0)
    return jnp.dot(rows, w_out, precision=HIGHEST) + result


def solution(mesh):
    placed = (
        P(("dp", "ctx")),
        P(),
        P(),
        P(None, "tp"),
        P(None, "tp"),
        P(),
        P(None, "tp"),
        P("tp"),
        P("tp"),
        P(None, "tp"),
        P(),
        P("tp"),
        P("tp"),
        P("tp", None),
    )
    return jax.shard_map(
        local, mesh=mesh, in_specs=placed, out_specs=P(("dp", "ctx", "tp"), None), check_vma=False
    )
```

```python
import jax
import jax.numpy as jnp
from jax import lax
from jax.sharding import PartitionSpec as P


CONV = 4
BLK = 256


HIGHEST = lax.Precision.HIGHEST
EPSILON = 1e-05


def shifted(value, axis, steps):
    count = lax.axis_size(axis)
    first, last = (max(0, -steps), min(count, count - steps))
    return lax.ppermute(value, axis, [(source, source + steps) for source in range(first, last)])


def causal_conv(padded, kernel):
    length = padded.shape[0] - kernel.shape[0] + 1
    output = jnp.zeros((length, padded.shape[1]), jnp.float32)
    for offset in range(kernel.shape[0]):
        output = output + kernel[offset][None, :] * padded[offset : offset + length]
    return output


def strand_local(joined_in, rim_rows, kernel, step_raw, step_bias, decay_rate, skip_gain,
                 gate, inner_local, state_size, head_dim, block_rows, backward):
    if backward:
        padded = jnp.concatenate([joined_in, rim_rows], axis=0)
        kernel = kernel[::-1]
    else:
        padded = jnp.concatenate([rim_rows, joined_in], axis=0)
    convolved = jax.nn.silu(causal_conv(padded, kernel))
    length = joined_in.shape[0]
    head_count = inner_local // head_dim
    block_count = length // block_rows
    values = convolved[:, :inner_local]
    b_in = convolved[:, inner_local : inner_local + state_size]
    c_out = convolved[:, inner_local + state_size :]
    step_size = jax.nn.softplus(step_raw + step_bias[None, :])
    log_step = -decay_rate[None, :] * step_size

    xs = values.reshape(block_count, block_rows, head_count, head_dim).transpose(0, 2, 1, 3)
    bs = b_in.reshape(block_count, block_rows, state_size)
    cs = c_out.reshape(block_count, block_rows, state_size)
    logs = log_step.reshape(block_count, block_rows, head_count).transpose(0, 2, 1)
    steps = step_size.reshape(block_count, block_rows, head_count).transpose(0, 2, 1)
    running = lax.cumsum(logs, axis=2, reverse=backward)
    totals = running[:, :, 0] if backward else running[:, :, -1]

    weighting = jnp.exp(totals[:, :, None] - running) * steps
    ends = jnp.einsum("bhj,bhjp,bjn->bhpn", weighting, xs, bs, precision=HIGHEST)
    order = list(range(block_count))
    if backward:
        order = order[::-1]
    prefix = {order[0]: jnp.zeros_like(ends[0])}
    for before, block in zip(order[:-1], order[1:]):
        prefix[block] = jnp.exp(totals[before])[:, None, None] * prefix[before] + ends[before]
    last = order[-1]
    memory = jnp.exp(totals[last])[:, None, None] * prefix[last] + ends[last]
    prefix = jnp.stack([prefix[block] for block in range(block_count)])
    offsets = lax.cumsum(totals, axis=0, reverse=backward) - totals
    total_log = jnp.sum(totals, axis=0)

    rows = jnp.arange(block_rows)[:, None]
    cols = jnp.arange(block_rows)[None, :]
    causal = ((rows <= cols) if backward else (rows >= cols))[None, None]
    spread = jnp.where(causal, running[:, :, :, None] - running[:, :, None, :], 0.0)
    weights = jnp.where(causal, jnp.exp(spread), 0.0)
    intersection = jnp.einsum("bin,bjn->bij", cs, bs, precision=HIGHEST)
    mixing = intersection[:, None] * weights * steps[:, :, None, :]
    inside = jnp.einsum("bhij,bhjp->bhip", mixing, xs, precision=HIGHEST)
    carried = jnp.einsum("bin,bhpn->bhip", cs, prefix, precision=HIGHEST)
    outputs = inside + carried * jnp.exp(running)[..., None]
    outputs = outputs + skip_gain[None, :, None, None] * xs
    outputs = outputs.transpose(0, 2, 1, 3).reshape(length, inner_local)
    reach = (offsets[:, :, None] + running).transpose(0, 2, 1).reshape(length, head_count)
    gate = jax.nn.silu(gate)
    return dict(outputs=outputs, c_out=c_out, reach=reach, memory=memory, total_log=total_log,
                gate=gate)


def finish_strand(parts, incoming):
    entering = jnp.einsum("tn,hpn->thp", parts["c_out"], incoming, precision=HIGHEST)
    entering = entering * jnp.exp(parts["reach"])[:, :, None]
    outputs = parts["outputs"] + entering.reshape(parts["outputs"].shape)
    return outputs * parts["gate"]


def relay(total_log, memory, axis, direction):
    count = lax.axis_size(axis)
    head_count, head_dim, state_size = memory.shape
    factor = jnp.broadcast_to(jnp.exp(total_log)[:, None, None], (head_count, 1, state_size))
    packed = shifted(jnp.concatenate([memory, factor], axis=1), axis, direction)
    distance = 1
    while distance < count:
        arrived = shifted(packed, axis, direction * distance)
        state = packed[:, :head_dim] + packed[:, head_dim:] * arrived[:, :head_dim]
        factor = packed[:, head_dim:] * arrived[:, head_dim:]
        packed = jnp.concatenate([state, factor], axis=1)
        distance *= 2
    return packed[:, :head_dim]


def local_body(
    nucleotides,
    complement,
    embedding,
    w_gate,
    w_value,
    w_state,
    w_step,
    step_bias,
    decay_rate,
    conv_value,
    conv_state,
    skip_gain,
    norm_weight,
    w_out,
):
    inner_local = w_gate.shape[1]
    state_size = w_state.shape[1] // 2
    head_count = step_bias.shape[0]
    head_dim = inner_local // head_count
    vocab_size = embedding.shape[0]
    table = jnp.concatenate([w_gate, w_value, w_state, w_step], axis=1)
    projected = jnp.dot(embedding, table, precision=HIGHEST)
    kernel = jnp.concatenate([conv_value, conv_state], axis=1)
    symbols = jnp.arange(vocab_size, dtype=jnp.int32)
    forward_match = nucleotides[:, None] == symbols[None, :]
    paired_ids = jnp.sum(jnp.where(forward_match, complement[None, :], 0), axis=1)
    reverse_hot = (paired_ids[:, None] == symbols[None, :]).astype(jnp.float32)
    forward_hot = forward_match.astype(jnp.float32)
    edge_rows = CONV - 1
    rim_forward_hot = shifted(forward_hot[-edge_rows:], "ctx", 1)
    rim_reverse_hot = shifted(reverse_hot[:edge_rows], "ctx", -1)
    split_step = 2 * inner_local + 2 * state_size
    conv_table = projected[:, inner_local:split_step]
    forward_rows = jnp.dot(forward_hot, projected, precision=HIGHEST)
    reverse_rows = jnp.dot(reverse_hot, projected, precision=HIGHEST)
    rim_forward = jnp.dot(rim_forward_hot, conv_table, precision=HIGHEST)
    rim_reverse = jnp.dot(rim_reverse_hot, conv_table, precision=HIGHEST)
    parts_f = strand_local(forward_rows[:, inner_local:split_step], rim_forward, kernel,
                           forward_rows[:, split_step:], step_bias, decay_rate, skip_gain,
                           forward_rows[:, :inner_local], inner_local, state_size, head_dim, BLK,
                           False)
    parts_r = strand_local(reverse_rows[:, inner_local:split_step], rim_reverse, kernel,
                           reverse_rows[:, split_step:], step_bias, decay_rate, skip_gain,
                           reverse_rows[:, :inner_local], inner_local, state_size, head_dim, BLK,
                           True)
    incoming_f = relay(parts_f["total_log"], parts_f["memory"], "ctx", 1)
    incoming_r = relay(parts_r["total_log"], parts_r["memory"], "ctx", -1)
    gated_f = finish_strand(parts_f, incoming_f)
    gated_r = finish_strand(parts_r, incoming_r)
    square_sums = lax.psum(
        (jnp.sum(gated_f * gated_f, axis=1), jnp.sum(gated_r * gated_r, axis=1)), "tp"
    )
    width_all = inner_local * lax.axis_size("tp")
    normed_f = (
        gated_f * lax.rsqrt(square_sums[0] / width_all + EPSILON)[:, None] * norm_weight[None, :]
    )
    normed_r = (
        gated_r * lax.rsqrt(square_sums[1] / width_all + EPSILON)[:, None] * norm_weight[None, :]
    )
    combined = normed_f + normed_r
    tp_count = lax.axis_size("tp")
    rows_each = combined.shape[0] // tp_count
    own = lax.axis_index("tp")
    result = None
    for turn in range(1, tp_count):
        target = (own + turn) % tp_count
        rows = lax.dynamic_slice_in_dim(combined, target * rows_each, rows_each, 0)
        partial = jnp.dot(rows, w_out, precision=HIGHEST)
        pairs = [(source, (source + turn) % tp_count) for source in range(tp_count)]
        arrived = lax.ppermute(partial, "tp", pairs)
        result = arrived if result is None else result + arrived
    rows = lax.dynamic_slice_in_dim(combined, own * rows_each, rows_each, 0)
    return jnp.dot(rows, w_out, precision=HIGHEST) + result


def solution(mesh):
    placed = (
        P(("dp", "ctx")),
        P(),
        P(),
        P(None, "tp"),
        P(None, "tp"),
        P(),
        P(None, "tp"),
        P("tp"),
        P("tp"),
        P(None, "tp"),
        P(),
        P("tp"),
        P("tp"),
        P("tp", None),
    )
    return jax.shard_map(
        local_body, mesh=mesh, in_specs=placed, out_specs=P(("dp", "ctx", "tp"), None), check_vma=False
    )
```

```python
import jax
import jax.numpy as jnp
from jax import lax
from jax.sharding import PartitionSpec as P


CONV = 4
BLK = 256


HIGHEST = lax.Precision.HIGHEST
HIGH = lax.Precision.HIGH
EPSILON = 1e-05


def shifted(value, axis, steps):
    count = lax.axis_size(axis)
    first, last = (max(0, -steps), min(count, count - steps))
    return lax.ppermute(value, axis, [(source, source + steps) for source in range(first, last)])


def causal_conv(padded, kernel):
    length = padded.shape[0] - kernel.shape[0] + 1
    output = jnp.zeros((length, padded.shape[1]), jnp.float32)
    for offset in range(kernel.shape[0]):
        output = output + kernel[offset][None, :] * padded[offset : offset + length]
    return output


def strand_local(joined_in, rim_rows, kernel, step_raw, step_bias, decay_rate, skip_gain,
                 gate, inner_local, state_size, head_dim, block_rows, backward):
    if backward:
        padded = jnp.concatenate([joined_in, rim_rows], axis=0)
        kernel = kernel[::-1]
    else:
        padded = jnp.concatenate([rim_rows, joined_in], axis=0)
    convolved = jax.nn.silu(causal_conv(padded, kernel))
    length = joined_in.shape[0]
    head_count = inner_local // head_dim
    block_count = length // block_rows
    values = convolved[:, :inner_local]
    b_in = convolved[:, inner_local : inner_local + state_size]
    c_out = convolved[:, inner_local + state_size :]
    step_size = jax.nn.softplus(step_raw + step_bias[None, :])
    log_step = -decay_rate[None, :] * step_size

    xs = values.reshape(block_count, block_rows, head_count, head_dim).transpose(0, 2, 1, 3)
    bs = b_in.reshape(block_count, block_rows, state_size)
    cs = c_out.reshape(block_count, block_rows, state_size)
    logs = log_step.reshape(block_count, block_rows, head_count).transpose(0, 2, 1)
    steps = step_size.reshape(block_count, block_rows, head_count).transpose(0, 2, 1)
    lower = jnp.arange(block_rows)[:, None]
    upper = jnp.arange(block_rows)[None, :]
    summing = ((lower >= upper) if backward else (lower <= upper)).astype(jnp.float32)
    running = jnp.einsum("bhj,ji->bhi", logs, summing, precision=HIGHEST)
    totals = running[:, :, 0] if backward else running[:, :, -1]

    weighting = jnp.exp(totals[:, :, None] - running) * steps
    ends = jnp.einsum("bhj,bhjp,bjn->bhpn", weighting, xs, bs, precision=HIGH)
    order = list(range(block_count))
    if backward:
        order = order[::-1]
    prefix = {order[0]: jnp.zeros_like(ends[0])}
    for before, block in zip(order[:-1], order[1:]):
        prefix[block] = jnp.exp(totals[before])[:, None, None] * prefix[before] + ends[before]
    last = order[-1]
    memory = jnp.exp(totals[last])[:, None, None] * prefix[last] + ends[last]
    prefix = jnp.stack([prefix[block] for block in range(block_count)])
    offsets = lax.cumsum(totals, axis=0, reverse=backward) - totals
    total_log = jnp.sum(totals, axis=0)

    rows = jnp.arange(block_rows)[:, None]
    cols = jnp.arange(block_rows)[None, :]
    causal = ((rows <= cols) if backward else (rows >= cols))[None, None]
    spread = jnp.where(causal, running[:, :, :, None] - running[:, :, None, :], 0.0)
    weights = jnp.where(causal, jnp.exp(spread), 0.0)
    intersection = jnp.einsum("bin,bjn->bij", cs, bs, precision=HIGHEST)
    mixing = intersection[:, None] * weights * steps[:, :, None, :]
    inside = jnp.einsum("bhij,bhjp->bhip", mixing, xs, precision=HIGHEST)
    carried = jnp.einsum("bin,bhpn->bhip", cs, prefix, precision=HIGHEST)
    outputs = inside + carried * jnp.exp(running)[..., None]
    outputs = outputs + skip_gain[None, :, None, None] * xs
    outputs = outputs.transpose(0, 2, 1, 3).reshape(length, inner_local)
    reach = (offsets[:, :, None] + running).transpose(0, 2, 1).reshape(length, head_count)
    gate = jax.nn.silu(gate)
    return dict(outputs=outputs, c_out=c_out, reach=reach, memory=memory, total_log=total_log,
                gate=gate)


def finish_strand(parts, incoming):
    entering = jnp.einsum("tn,hpn->thp", parts["c_out"], incoming, precision=HIGH)
    entering = entering * jnp.exp(parts["reach"])[:, :, None]
    outputs = parts["outputs"] + entering.reshape(parts["outputs"].shape)
    return outputs * parts["gate"]


def relay(total_log, memory, axis, direction):
    count = lax.axis_size(axis)
    head_count, head_dim, state_size = memory.shape
    factor = jnp.broadcast_to(jnp.exp(total_log)[:, None, None], (head_count, 1, state_size))
    packed = shifted(jnp.concatenate([memory, factor], axis=1), axis, direction)
    distance = 1
    while distance < count:
        arrived = shifted(packed, axis, direction * distance)
        state = packed[:, :head_dim] + packed[:, head_dim:] * arrived[:, :head_dim]
        factor = packed[:, head_dim:] * arrived[:, head_dim:]
        packed = jnp.concatenate([state, factor], axis=1)
        distance *= 2
    return packed[:, :head_dim]


def local_body(
    nucleotides,
    complement,
    embedding,
    w_gate,
    w_value,
    w_state,
    w_step,
    step_bias,
    decay_rate,
    conv_value,
    conv_state,
    skip_gain,
    norm_weight,
    w_out,
):
    inner_local = w_gate.shape[1]
    state_size = w_state.shape[1] // 2
    head_count = step_bias.shape[0]
    head_dim = inner_local // head_count
    vocab_size = embedding.shape[0]
    table = jnp.concatenate([w_gate, w_value, w_state, w_step], axis=1)
    projected = jnp.dot(embedding, table, precision=HIGH)
    kernel = jnp.concatenate([conv_value, conv_state], axis=1)
    symbols = jnp.arange(vocab_size, dtype=jnp.int32)
    forward_match = nucleotides[:, None] == symbols[None, :]
    paired_ids = jnp.sum(jnp.where(forward_match, complement[None, :], 0), axis=1)
    reverse_hot = (paired_ids[:, None] == symbols[None, :]).astype(jnp.float32)
    forward_hot = forward_match.astype(jnp.float32)
    edge_rows = CONV - 1
    rim_forward_hot = shifted(forward_hot[-edge_rows:], "ctx", 1)
    rim_reverse_hot = shifted(reverse_hot[:edge_rows], "ctx", -1)
    split_step = 2 * inner_local + 2 * state_size
    conv_table = projected[:, inner_local:split_step]
    forward_rows = jnp.dot(forward_hot, projected, precision=HIGHEST)
    reverse_rows = jnp.dot(reverse_hot, projected, precision=HIGHEST)
    rim_forward = jnp.dot(rim_forward_hot, conv_table, precision=HIGHEST)
    rim_reverse = jnp.dot(rim_reverse_hot, conv_table, precision=HIGHEST)
    parts_f = strand_local(forward_rows[:, inner_local:split_step], rim_forward, kernel,
                           forward_rows[:, split_step:], step_bias, decay_rate, skip_gain,
                           forward_rows[:, :inner_local], inner_local, state_size, head_dim, BLK,
                           False)
    parts_r = strand_local(reverse_rows[:, inner_local:split_step], rim_reverse, kernel,
                           reverse_rows[:, split_step:], step_bias, decay_rate, skip_gain,
                           reverse_rows[:, :inner_local], inner_local, state_size, head_dim, BLK,
                           True)
    incoming_f = relay(parts_f["total_log"], parts_f["memory"], "ctx", 1)
    incoming_r = relay(parts_r["total_log"], parts_r["memory"], "ctx", -1)
    gated_f = finish_strand(parts_f, incoming_f)
    gated_r = finish_strand(parts_r, incoming_r)
    square_sums = lax.psum(
        (jnp.sum(gated_f * gated_f, axis=1), jnp.sum(gated_r * gated_r, axis=1)), "tp"
    )
    width_all = inner_local * lax.axis_size("tp")
    normed_f = (
        gated_f * lax.rsqrt(square_sums[0] / width_all + EPSILON)[:, None] * norm_weight[None, :]
    )
    normed_r = (
        gated_r * lax.rsqrt(square_sums[1] / width_all + EPSILON)[:, None] * norm_weight[None, :]
    )
    combined = normed_f + normed_r
    tp_count = lax.axis_size("tp")
    rows_each = combined.shape[0] // tp_count
    own = lax.axis_index("tp")
    result = None
    for turn in range(1, tp_count):
        target = (own + turn) % tp_count
        rows = lax.dynamic_slice_in_dim(combined, target * rows_each, rows_each, 0)
        partial = jnp.dot(rows, w_out, precision=HIGH)
        pairs = [(source, (source + turn) % tp_count) for source in range(tp_count)]
        arrived = lax.ppermute(partial, "tp", pairs)
        result = arrived if result is None else result + arrived
    rows = lax.dynamic_slice_in_dim(combined, own * rows_each, rows_each, 0)
    return jnp.dot(rows, w_out, precision=HIGH) + result


def solution(mesh):
    placed = (
        P(("dp", "ctx")),
        P(),
        P(),
        P(None, "tp"),
        P(None, "tp"),
        P(),
        P(None, "tp"),
        P("tp"),
        P("tp"),
        P(None, "tp"),
        P(),
        P("tp"),
        P("tp"),
        P("tp", None),
    )
    return jax.shard_map(
        local_body, mesh=mesh, in_specs=placed, out_specs=P(("dp", "ctx", "tp"), None), check_vma=False
    )
```

```python
import jax
import jax.numpy as jnp
from jax import lax
from jax.sharding import PartitionSpec as P


CONV = 4
BLK = 256


HIGHEST = lax.Precision.HIGHEST
HIGH = lax.Precision.HIGH
EPSILON = 1e-05


def shifted(value, axis, steps):
    count = lax.axis_size(axis)
    first, last = (max(0, -steps), min(count, count - steps))
    return lax.ppermute(value, axis, [(source, source + steps) for source in range(first, last)])


def strand_local(hot, rim_hot, kernel, conv_table, step_table, gate_table, step_bias,
                 decay_rate, skip_gain, inner_local, state_size, head_dim, block_rows, backward):
    if backward:
        padded = jnp.concatenate([hot, rim_hot], axis=0)
        kernel = kernel[::-1]
    else:
        padded = jnp.concatenate([rim_hot, hot], axis=0)
    length, vocab_size = hot.shape
    taps = kernel.shape[0]
    head_count = inner_local // head_dim
    block_count = length // block_rows
    window = jnp.concatenate([padded[tap : tap + length] for tap in range(taps)], axis=1)
    window = window.reshape(block_count, block_rows, taps * vocab_size)
    tap_table = (kernel[:, None, :] * conv_table[None, :, :]).reshape(taps * vocab_size, -1)
    value_table = tap_table[:, :inner_local].reshape(-1, head_count, head_dim)
    xs = jax.nn.silu(jnp.einsum("btk,khp->bhtp", window, value_table, precision=HIGHEST))
    bs = jax.nn.silu(jnp.einsum("btk,kn->btn", window,
                                tap_table[:, inner_local : inner_local + state_size],
                                precision=HIGHEST))
    cs = jax.nn.silu(jnp.einsum("btk,kn->btn", window, tap_table[:, inner_local + state_size :],
                                precision=HIGHEST))
    blocks_hot = hot.reshape(block_count, block_rows, vocab_size)
    step_raw = jnp.einsum("btk,kh->bht", blocks_hot, step_table, precision=HIGHEST)
    steps = jax.nn.softplus(step_raw + step_bias[None, :, None])
    logs = -decay_rate[None, :, None] * steps
    c_out = cs.reshape(length, state_size)
    gate = jnp.dot(hot, gate_table, precision=HIGHEST)
    lower = jnp.arange(block_rows)[:, None]
    upper = jnp.arange(block_rows)[None, :]
    summing = ((lower >= upper) if backward else (lower <= upper)).astype(jnp.float32)
    running = jnp.einsum("bhj,ji->bhi", logs, summing, precision=HIGHEST)
    totals = running[:, :, 0] if backward else running[:, :, -1]

    weighting = jnp.exp(totals[:, :, None] - running) * steps
    ends = jnp.einsum("bhj,bhjp,bjn->bhpn", weighting, xs, bs, precision=HIGH)
    order = list(range(block_count))
    if backward:
        order = order[::-1]
    prefix = {order[0]: jnp.zeros_like(ends[0])}
    for before, block in zip(order[:-1], order[1:]):
        prefix[block] = jnp.exp(totals[before])[:, None, None] * prefix[before] + ends[before]
    last = order[-1]
    memory = jnp.exp(totals[last])[:, None, None] * prefix[last] + ends[last]
    prefix = jnp.stack([prefix[block] for block in range(block_count)])
    offsets = lax.cumsum(totals, axis=0, reverse=backward) - totals
    total_log = jnp.sum(totals, axis=0)

    rows = jnp.arange(block_rows)[:, None]
    cols = jnp.arange(block_rows)[None, :]
    causal = ((rows <= cols) if backward else (rows >= cols))[None, None]
    spread = jnp.where(causal, running[:, :, :, None] - running[:, :, None, :], 0.0)
    weights = jnp.where(causal, jnp.exp(spread), 0.0)
    intersection = jnp.einsum("bin,bjn->bij", cs, bs, precision=HIGHEST)
    mixing = intersection[:, None] * weights * steps[:, :, None, :]
    inside = jnp.einsum("bhij,bhjp->bhip", mixing, xs, precision=HIGHEST)
    carried = jnp.einsum("bin,bhpn->bhip", cs, prefix, precision=HIGHEST)
    outputs = inside + carried * jnp.exp(running)[..., None]
    outputs = outputs + skip_gain[None, :, None, None] * xs
    outputs = outputs.transpose(0, 2, 1, 3).reshape(length, inner_local)
    reach = (offsets[:, :, None] + running).transpose(0, 2, 1).reshape(length, head_count)
    gate = jax.nn.silu(gate)
    return dict(outputs=outputs, c_out=c_out, reach=reach, memory=memory, total_log=total_log,
                gate=gate)


def finish_strand(parts, incoming):
    entering = jnp.einsum("tn,hpn->thp", parts["c_out"], incoming, precision=HIGH)
    entering = entering * jnp.exp(parts["reach"])[:, :, None]
    outputs = parts["outputs"] + entering.reshape(parts["outputs"].shape)
    return outputs * parts["gate"]


def relay(total_log, memory, axis, direction):
    count = lax.axis_size(axis)
    head_count, head_dim, state_size = memory.shape
    factor = jnp.broadcast_to(jnp.exp(total_log)[:, None, None], (head_count, 1, state_size))
    packed = shifted(jnp.concatenate([memory, factor], axis=1), axis, direction)
    distance = 1
    while distance < count:
        arrived = shifted(packed, axis, direction * distance)
        state = packed[:, :head_dim] + packed[:, head_dim:] * arrived[:, :head_dim]
        factor = packed[:, head_dim:] * arrived[:, head_dim:]
        packed = jnp.concatenate([state, factor], axis=1)
        distance *= 2
    return packed[:, :head_dim]


def local_body(
    nucleotides,
    complement,
    embedding,
    w_gate,
    w_value,
    w_state,
    w_step,
    step_bias,
    decay_rate,
    conv_value,
    conv_state,
    skip_gain,
    norm_weight,
    w_out,
):
    inner_local = w_gate.shape[1]
    state_size = w_state.shape[1] // 2
    head_count = step_bias.shape[0]
    head_dim = inner_local // head_count
    vocab_size = embedding.shape[0]
    table = jnp.concatenate([w_gate, w_value, w_state, w_step], axis=1)
    projected = jnp.dot(embedding, table, precision=HIGH)
    kernel = jnp.concatenate([conv_value, conv_state], axis=1)
    symbols = jnp.arange(vocab_size, dtype=jnp.int32)
    forward_match = nucleotides[:, None] == symbols[None, :]
    paired_ids = jnp.sum(jnp.where(forward_match, complement[None, :], 0), axis=1)
    reverse_hot = (paired_ids[:, None] == symbols[None, :]).astype(jnp.float32)
    forward_hot = forward_match.astype(jnp.float32)
    edge_rows = CONV - 1
    rim_forward_hot = shifted(forward_hot[-edge_rows:], "ctx", 1)
    rim_reverse_hot = shifted(reverse_hot[:edge_rows], "ctx", -1)
    split_step = 2 * inner_local + 2 * state_size
    conv_table = projected[:, inner_local:split_step]
    step_table = projected[:, split_step:]
    gate_table = projected[:, :inner_local]
    parts_f = strand_local(forward_hot, rim_forward_hot, kernel, conv_table, step_table,
                           gate_table, step_bias, decay_rate, skip_gain, inner_local, state_size,
                           head_dim, BLK, False)
    parts_r = strand_local(reverse_hot, rim_reverse_hot, kernel, conv_table, step_table,
                           gate_table, step_bias, decay_rate, skip_gain, inner_local, state_size,
                           head_dim, BLK, True)
    incoming_f = relay(parts_f["total_log"], parts_f["memory"], "ctx", 1)
    incoming_r = relay(parts_r["total_log"], parts_r["memory"], "ctx", -1)
    gated_f = finish_strand(parts_f, incoming_f)
    gated_r = finish_strand(parts_r, incoming_r)
    square_sums = lax.psum(
        (jnp.sum(gated_f * gated_f, axis=1), jnp.sum(gated_r * gated_r, axis=1)), "tp"
    )
    width_all = inner_local * lax.axis_size("tp")
    normed_f = (
        gated_f * lax.rsqrt(square_sums[0] / width_all + EPSILON)[:, None] * norm_weight[None, :]
    )
    normed_r = (
        gated_r * lax.rsqrt(square_sums[1] / width_all + EPSILON)[:, None] * norm_weight[None, :]
    )
    combined = normed_f + normed_r
    tp_count = lax.axis_size("tp")
    rows_each = combined.shape[0] // tp_count
    own = lax.axis_index("tp")
    result = None
    for turn in range(1, tp_count):
        target = (own + turn) % tp_count
        rows = lax.dynamic_slice_in_dim(combined, target * rows_each, rows_each, 0)
        partial = jnp.dot(rows, w_out, precision=HIGH)
        pairs = [(source, (source + turn) % tp_count) for source in range(tp_count)]
        arrived = lax.ppermute(partial, "tp", pairs)
        result = arrived if result is None else result + arrived
    rows = lax.dynamic_slice_in_dim(combined, own * rows_each, rows_each, 0)
    return jnp.dot(rows, w_out, precision=HIGH) + result


def solution(mesh):
    placed = (
        P(("dp", "ctx")),
        P(),
        P(),
        P(None, "tp"),
        P(None, "tp"),
        P(),
        P(None, "tp"),
        P("tp"),
        P("tp"),
        P(None, "tp"),
        P(),
        P("tp"),
        P("tp"),
        P("tp", None),
    )
    return jax.shard_map(
        local_body, mesh=mesh, in_specs=placed, out_specs=P(("dp", "ctx", "tp"), None), check_vma=False
    )
```

```python
import jax
import jax.numpy as jnp
from jax import lax
from jax.sharding import PartitionSpec as P


CONV = 4
BLK = 256


HIGHEST = lax.Precision.HIGHEST
HIGH = lax.Precision.HIGH
EPSILON = 1e-05


def shifted(value, axis, steps):
    count = lax.axis_size(axis)
    first, last = (max(0, -steps), min(count, count - steps))
    return lax.ppermute(value, axis, [(source, source + steps) for source in range(first, last)])


def causal_conv(padded, kernel):
    length = padded.shape[0] - kernel.shape[0] + 1
    output = jnp.zeros((length, padded.shape[1]), jnp.float32)
    for offset in range(kernel.shape[0]):
        output = output + kernel[offset][None, :] * padded[offset : offset + length]
    return output


def strand_local(joined_in, rim_rows, kernel, step_raw, step_bias, decay_rate, skip_gain,
                 gate, inner_local, state_size, head_dim, block_rows, backward):
    if backward:
        padded = jnp.concatenate([joined_in, rim_rows], axis=0)
        kernel = kernel[::-1]
    else:
        padded = jnp.concatenate([rim_rows, joined_in], axis=0)
    convolved = jax.nn.silu(causal_conv(padded, kernel))
    length = joined_in.shape[0]
    head_count = inner_local // head_dim
    block_count = length // block_rows
    values = convolved[:, :inner_local]
    b_in = convolved[:, inner_local : inner_local + state_size]
    c_out = convolved[:, inner_local + state_size :]
    step_size = jax.nn.softplus(step_raw + step_bias[None, :])
    log_step = -decay_rate[None, :] * step_size

    xs = values.reshape(block_count, block_rows, head_count, head_dim).transpose(0, 2, 1, 3)
    bs = b_in.reshape(block_count, block_rows, state_size)
    cs = c_out.reshape(block_count, block_rows, state_size)
    logs = log_step.reshape(block_count, block_rows, head_count).transpose(0, 2, 1)
    steps = step_size.reshape(block_count, block_rows, head_count).transpose(0, 2, 1)
    lower = jnp.arange(block_rows)[:, None]
    upper = jnp.arange(block_rows)[None, :]
    summing = ((lower >= upper) if backward else (lower <= upper)).astype(jnp.float32)
    running = jnp.einsum("bhj,ji->bhi", logs, summing, precision=HIGHEST)
    totals = running[:, :, 0] if backward else running[:, :, -1]

    weighting = jnp.exp(totals[:, :, None] - running) * steps
    ends = jnp.einsum("bhj,bhjp,bjn->bhpn", weighting, xs, bs, precision=HIGH)
    order = list(range(block_count))
    if backward:
        order = order[::-1]
    prefix = {order[0]: jnp.zeros_like(ends[0])}
    for before, block in zip(order[:-1], order[1:]):
        prefix[block] = jnp.exp(totals[before])[:, None, None] * prefix[before] + ends[before]
    last = order[-1]
    memory = jnp.exp(totals[last])[:, None, None] * prefix[last] + ends[last]
    prefix = jnp.stack([prefix[block] for block in range(block_count)])
    offsets = lax.cumsum(totals, axis=0, reverse=backward) - totals
    total_log = jnp.sum(totals, axis=0)

    rows = jnp.arange(block_rows)[:, None]
    cols = jnp.arange(block_rows)[None, :]
    causal = ((rows <= cols) if backward else (rows >= cols))[None, None]
    spread = jnp.where(causal, running[:, :, :, None] - running[:, :, None, :], 0.0)
    weights = jnp.where(causal, jnp.exp(spread), 0.0)
    intersection = jnp.einsum("bin,bjn->bij", cs, bs, precision=HIGHEST)
    mixing = intersection[:, None] * weights * steps[:, :, None, :]
    inside = jnp.einsum("bhij,bhjp->bhip", mixing, xs, precision=HIGHEST)
    carried = jnp.einsum("bin,bhpn->bhip", cs, prefix, precision=HIGHEST)
    outputs = inside + carried * jnp.exp(running)[..., None]
    outputs = outputs + skip_gain[None, :, None, None] * xs
    outputs = outputs.transpose(0, 2, 1, 3).reshape(length, inner_local)
    reach = (offsets[:, :, None] + running).transpose(0, 2, 1).reshape(length, head_count)
    gate = jax.nn.silu(gate)
    return dict(outputs=outputs, c_out=c_out, reach=reach, memory=memory, total_log=total_log,
                gate=gate)


def finish_strand(parts, incoming):
    entering = jnp.einsum("tn,hpn->thp", parts["c_out"], incoming, precision=HIGH)
    entering = entering * jnp.exp(parts["reach"])[:, :, None]
    outputs = parts["outputs"] + entering.reshape(parts["outputs"].shape)
    return outputs * parts["gate"]


def relay(total_log, memory, axis, direction):
    count = lax.axis_size(axis)
    head_count, head_dim, state_size = memory.shape
    factor = jnp.broadcast_to(jnp.exp(total_log)[:, None, None], (head_count, 1, state_size))
    own = jnp.concatenate([memory, factor], axis=1)
    near = shifted(own, axis, direction)
    far = shifted(own, axis, 2 * direction)
    state = near[:, :head_dim] + near[:, head_dim:] * far[:, :head_dim]
    packed = jnp.concatenate([state, near[:, head_dim:] * far[:, head_dim:]], axis=1)
    distance = 2
    while distance < count:
        arrived = shifted(packed, axis, direction * distance)
        state = packed[:, :head_dim] + packed[:, head_dim:] * arrived[:, :head_dim]
        factor = packed[:, head_dim:] * arrived[:, head_dim:]
        packed = jnp.concatenate([state, factor], axis=1)
        distance *= 2
    return packed[:, :head_dim]


def local_body(
    nucleotides,
    complement,
    embedding,
    w_gate,
    w_value,
    w_state,
    w_step,
    step_bias,
    decay_rate,
    conv_value,
    conv_state,
    skip_gain,
    norm_weight,
    w_out,
):
    inner_local = w_gate.shape[1]
    state_size = w_state.shape[1] // 2
    head_count = step_bias.shape[0]
    head_dim = inner_local // head_count
    vocab_size = embedding.shape[0]
    table = jnp.concatenate([w_gate, w_value, w_state, w_step], axis=1)
    projected = jnp.dot(embedding, table, precision=HIGH)
    kernel = jnp.concatenate([conv_value, conv_state], axis=1)
    symbols = jnp.arange(vocab_size, dtype=jnp.int32)
    forward_match = nucleotides[:, None] == symbols[None, :]
    paired_ids = jnp.sum(jnp.where(forward_match, complement[None, :], 0), axis=1)
    reverse_hot = (paired_ids[:, None] == symbols[None, :]).astype(jnp.float32)
    forward_hot = forward_match.astype(jnp.float32)
    edge_rows = CONV - 1
    rim_forward_hot = shifted(forward_hot[-edge_rows:], "ctx", 1)
    rim_reverse_hot = shifted(reverse_hot[:edge_rows], "ctx", -1)
    split_step = 2 * inner_local + 2 * state_size
    conv_table = projected[:, inner_local:split_step]
    forward_rows = jnp.dot(forward_hot, projected, precision=HIGHEST)
    reverse_rows = jnp.dot(reverse_hot, projected, precision=HIGHEST)
    rim_forward = jnp.dot(rim_forward_hot, conv_table, precision=HIGHEST)
    rim_reverse = jnp.dot(rim_reverse_hot, conv_table, precision=HIGHEST)
    parts_f = strand_local(forward_rows[:, inner_local:split_step], rim_forward, kernel,
                           forward_rows[:, split_step:], step_bias, decay_rate, skip_gain,
                           forward_rows[:, :inner_local], inner_local, state_size, head_dim, BLK,
                           False)
    parts_r = strand_local(reverse_rows[:, inner_local:split_step], rim_reverse, kernel,
                           reverse_rows[:, split_step:], step_bias, decay_rate, skip_gain,
                           reverse_rows[:, :inner_local], inner_local, state_size, head_dim, BLK,
                           True)
    incoming_f = relay(parts_f["total_log"], parts_f["memory"], "ctx", 1)
    incoming_r = relay(parts_r["total_log"], parts_r["memory"], "ctx", -1)
    gated_f = finish_strand(parts_f, incoming_f)
    gated_r = finish_strand(parts_r, incoming_r)
    square_sums = lax.psum(
        (jnp.sum(gated_f * gated_f, axis=1), jnp.sum(gated_r * gated_r, axis=1)), "tp"
    )
    width_all = inner_local * lax.axis_size("tp")
    normed_f = (
        gated_f * lax.rsqrt(square_sums[0] / width_all + EPSILON)[:, None] * norm_weight[None, :]
    )
    normed_r = (
        gated_r * lax.rsqrt(square_sums[1] / width_all + EPSILON)[:, None] * norm_weight[None, :]
    )
    combined = normed_f + normed_r
    tp_count = lax.axis_size("tp")
    rows_each = combined.shape[0] // tp_count
    own = lax.axis_index("tp")
    result = None
    for turn in range(1, tp_count):
        target = (own + turn) % tp_count
        rows = lax.dynamic_slice_in_dim(combined, target * rows_each, rows_each, 0)
        partial = jnp.dot(rows, w_out, precision=HIGH)
        pairs = [(source, (source + turn) % tp_count) for source in range(tp_count)]
        arrived = lax.ppermute(partial, "tp", pairs)
        result = arrived if result is None else result + arrived
    rows = lax.dynamic_slice_in_dim(combined, own * rows_each, rows_each, 0)
    return jnp.dot(rows, w_out, precision=HIGH) + result


def solution(mesh):
    placed = (
        P(("dp", "ctx")),
        P(),
        P(),
        P(None, "tp"),
        P(None, "tp"),
        P(),
        P(None, "tp"),
        P("tp"),
        P("tp"),
        P(None, "tp"),
        P(),
        P("tp"),
        P("tp"),
        P("tp", None),
    )
    return jax.shard_map(
        local_body, mesh=mesh, in_specs=placed, out_specs=P(("dp", "ctx", "tp"), None), check_vma=False
    )
```

```python
import jax
import jax.numpy as jnp
from jax import lax
from jax.sharding import PartitionSpec as P


CONV = 4
BLK = 256


HIGHEST = lax.Precision.HIGHEST
HIGH = lax.Precision.HIGH
EPSILON = 1e-05


def shifted(value, axis, steps):
    count = lax.axis_size(axis)
    first, last = (max(0, -steps), min(count, count - steps))
    return lax.ppermute(value, axis, [(source, source + steps) for source in range(first, last)])


def causal_conv(padded, kernel):
    length = padded.shape[0] - kernel.shape[0] + 1
    output = jnp.zeros((length, padded.shape[1]), jnp.float32)
    for offset in range(kernel.shape[0]):
        output = output + kernel[offset][None, :] * padded[offset : offset + length]
    return output


def strand_local(joined_in, rim_rows, kernel, step_raw, step_bias, decay_rate, skip_gain,
                 gate, inner_local, state_size, head_dim, block_rows, backward):
    if backward:
        padded = jnp.concatenate([joined_in, rim_rows], axis=0)
        kernel = kernel[::-1]
    else:
        padded = jnp.concatenate([rim_rows, joined_in], axis=0)
    convolved = jax.nn.silu(causal_conv(padded, kernel))
    length = joined_in.shape[0]
    head_count = inner_local // head_dim
    block_count = length // block_rows
    values = convolved[:, :inner_local]
    b_in = convolved[:, inner_local : inner_local + state_size]
    c_out = convolved[:, inner_local + state_size :]
    step_size = jax.nn.softplus(step_raw + step_bias[None, :])
    log_step = -decay_rate[None, :] * step_size

    xs = values.reshape(block_count, block_rows, head_count, head_dim).transpose(0, 2, 1, 3)
    bs = b_in.reshape(block_count, block_rows, state_size)
    cs = c_out.reshape(block_count, block_rows, state_size)
    logs = log_step.reshape(block_count, block_rows, head_count).transpose(0, 2, 1)
    steps = step_size.reshape(block_count, block_rows, head_count).transpose(0, 2, 1)
    lower = jnp.arange(block_rows)[:, None]
    upper = jnp.arange(block_rows)[None, :]
    summing = ((lower >= upper) if backward else (lower <= upper)).astype(jnp.float32)
    running = jnp.einsum("bhj,ji->bhi", logs, summing, precision=HIGHEST)
    totals = running[:, :, 0] if backward else running[:, :, -1]

    weighting = jnp.exp(totals[:, :, None] - running) * steps
    ends = jnp.einsum("bhj,bhjp,bjn->bhpn", weighting, xs, bs, precision=HIGH)
    order = list(range(block_count))
    if backward:
        order = order[::-1]
    prefix = {order[0]: jnp.zeros_like(ends[0])}
    for before, block in zip(order[:-1], order[1:]):
        prefix[block] = jnp.exp(totals[before])[:, None, None] * prefix[before] + ends[before]
    last = order[-1]
    memory = jnp.exp(totals[last])[:, None, None] * prefix[last] + ends[last]
    prefix = jnp.stack([prefix[block] for block in range(block_count)])
    offsets = lax.cumsum(totals, axis=0, reverse=backward) - totals
    total_log = jnp.sum(totals, axis=0)

    rows = jnp.arange(block_rows)[:, None]
    cols = jnp.arange(block_rows)[None, :]
    causal = ((rows <= cols) if backward else (rows >= cols))[None, None]
    spread = jnp.where(causal, running[:, :, :, None] - running[:, :, None, :], 0.0)
    weights = jnp.where(causal, jnp.exp(spread), 0.0)
    intersection = jnp.einsum("bin,bjn->bij", cs, bs, precision=HIGHEST)
    mixing = intersection[:, None] * weights * steps[:, :, None, :]
    inside = jnp.einsum("bhij,bhjp->bhip", mixing, xs, precision=HIGHEST)
    carried = jnp.einsum("bin,bhpn->bhip", cs, prefix, precision=HIGHEST)
    outputs = inside + carried * jnp.exp(running)[..., None]
    outputs = outputs + skip_gain[None, :, None, None] * xs
    outputs = outputs.transpose(0, 2, 1, 3).reshape(length, inner_local)
    reach = (offsets[:, :, None] + running).transpose(0, 2, 1).reshape(length, head_count)
    gate = jax.nn.silu(gate)
    return dict(outputs=outputs, c_out=c_out, reach=reach, memory=memory, total_log=total_log,
                gate=gate)


def finish_strand(parts, incoming):
    entering = jnp.einsum("tn,hpn->thp", parts["c_out"], incoming, precision=HIGH)
    entering = entering * jnp.exp(parts["reach"])[:, :, None]
    outputs = parts["outputs"] + entering.reshape(parts["outputs"].shape)
    return outputs * parts["gate"]


def relay(total_log, memory, axis, direction):
    count = lax.axis_size(axis)
    head_count, head_dim, state_size = memory.shape
    factor = jnp.broadcast_to(jnp.exp(total_log)[:, None, None], (head_count, 1, state_size))
    own = jnp.concatenate([memory, factor], axis=1)
    state = None
    window = 0
    fan = 2
    while window < count - 1:
        reach = max(window, 1)
        fan_out = min(fan, -(-(count - 1 - window) // reach))
        arrived = [shifted(own, axis, direction * reach * step) for step in range(1, fan_out + 1)]
        for packet in arrived:
            if state is None:
                state = packet[:, :head_dim]
                factor = packet[:, head_dim:]
            else:
                state = state + factor * packet[:, :head_dim]
                factor = factor * packet[:, head_dim:]
        window = window + reach * fan_out
        own = jnp.concatenate([state, factor], axis=1)
    return state


def local_body(
    nucleotides,
    complement,
    embedding,
    w_gate,
    w_value,
    w_state,
    w_step,
    step_bias,
    decay_rate,
    conv_value,
    conv_state,
    skip_gain,
    norm_weight,
    w_out,
):
    inner_local = w_gate.shape[1]
    state_size = w_state.shape[1] // 2
    head_count = step_bias.shape[0]
    head_dim = inner_local // head_count
    vocab_size = embedding.shape[0]
    table = jnp.concatenate([w_gate, w_value, w_state, w_step], axis=1)
    projected = jnp.dot(embedding, table, precision=HIGH)
    kernel = jnp.concatenate([conv_value, conv_state], axis=1)
    symbols = jnp.arange(vocab_size, dtype=jnp.int32)
    forward_match = nucleotides[:, None] == symbols[None, :]
    paired_ids = jnp.sum(jnp.where(forward_match, complement[None, :], 0), axis=1)
    reverse_hot = (paired_ids[:, None] == symbols[None, :]).astype(jnp.float32)
    forward_hot = forward_match.astype(jnp.float32)
    edge_rows = CONV - 1
    rim_forward_hot = shifted(forward_hot[-edge_rows:], "ctx", 1)
    rim_reverse_hot = shifted(reverse_hot[:edge_rows], "ctx", -1)
    split_step = 2 * inner_local + 2 * state_size
    conv_table = projected[:, inner_local:split_step]
    forward_rows = jnp.dot(forward_hot, projected, precision=HIGHEST)
    reverse_rows = jnp.dot(reverse_hot, projected, precision=HIGHEST)
    rim_forward = jnp.dot(rim_forward_hot, conv_table, precision=HIGHEST)
    rim_reverse = jnp.dot(rim_reverse_hot, conv_table, precision=HIGHEST)
    parts_f = strand_local(forward_rows[:, inner_local:split_step], rim_forward, kernel,
                           forward_rows[:, split_step:], step_bias, decay_rate, skip_gain,
                           forward_rows[:, :inner_local], inner_local, state_size, head_dim, BLK,
                           False)
    parts_r = strand_local(reverse_rows[:, inner_local:split_step], rim_reverse, kernel,
                           reverse_rows[:, split_step:], step_bias, decay_rate, skip_gain,
                           reverse_rows[:, :inner_local], inner_local, state_size, head_dim, BLK,
                           True)
    incoming_f = relay(parts_f["total_log"], parts_f["memory"], "ctx", 1)
    incoming_r = relay(parts_r["total_log"], parts_r["memory"], "ctx", -1)
    gated_f = finish_strand(parts_f, incoming_f)
    gated_r = finish_strand(parts_r, incoming_r)
    square_sums = lax.psum(
        (jnp.sum(gated_f * gated_f, axis=1), jnp.sum(gated_r * gated_r, axis=1)), "tp"
    )
    width_all = inner_local * lax.axis_size("tp")
    normed_f = (
        gated_f * lax.rsqrt(square_sums[0] / width_all + EPSILON)[:, None] * norm_weight[None, :]
    )
    normed_r = (
        gated_r * lax.rsqrt(square_sums[1] / width_all + EPSILON)[:, None] * norm_weight[None, :]
    )
    combined = normed_f + normed_r
    tp_count = lax.axis_size("tp")
    rows_each = combined.shape[0] // tp_count
    own = lax.axis_index("tp")
    result = None
    for turn in range(1, tp_count):
        target = (own + turn) % tp_count
        rows = lax.dynamic_slice_in_dim(combined, target * rows_each, rows_each, 0)
        partial = jnp.dot(rows, w_out, precision=HIGH)
        pairs = [(source, (source + turn) % tp_count) for source in range(tp_count)]
        arrived = lax.ppermute(partial, "tp", pairs)
        result = arrived if result is None else result + arrived
    rows = lax.dynamic_slice_in_dim(combined, own * rows_each, rows_each, 0)
    return jnp.dot(rows, w_out, precision=HIGH) + result


def solution(mesh):
    placed = (
        P(("dp", "ctx")),
        P(),
        P(),
        P(None, "tp"),
        P(None, "tp"),
        P(),
        P(None, "tp"),
        P("tp"),
        P("tp"),
        P(None, "tp"),
        P(),
        P("tp"),
        P("tp"),
        P("tp", None),
    )
    return jax.shard_map(
        local_body, mesh=mesh, in_specs=placed, out_specs=P(("dp", "ctx", "tp"), None), check_vma=False
    )
```

```python
import jax
import jax.numpy as jnp
from jax import lax
from jax.sharding import PartitionSpec as P


CONV = 4
BLK = 256


HIGHEST = lax.Precision.HIGHEST
HIGH = lax.Precision.HIGH
EPSILON = 1e-05


def shifted(value, axis, steps):
    count = lax.axis_size(axis)
    first, last = (max(0, -steps), min(count, count - steps))
    return lax.ppermute(value, axis, [(source, source + steps) for source in range(first, last)])


def causal_conv(padded, kernel):
    length = padded.shape[0] - kernel.shape[0] + 1
    output = jnp.zeros((length, padded.shape[1]), jnp.float32)
    for offset in range(kernel.shape[0]):
        output = output + kernel[offset][None, :] * padded[offset : offset + length]
    return output


def strand_local(joined_in, rim_rows, kernel, step_raw, step_bias, decay_rate, skip_gain,
                 gate, inner_local, state_size, head_dim, block_rows, backward):
    if backward:
        padded = jnp.concatenate([joined_in, rim_rows], axis=0)
        kernel = kernel[::-1]
    else:
        padded = jnp.concatenate([rim_rows, joined_in], axis=0)
    convolved = jax.nn.silu(causal_conv(padded, kernel))
    length = joined_in.shape[0]
    head_count = inner_local // head_dim
    block_count = length // block_rows
    values = convolved[:, :inner_local]
    b_in = convolved[:, inner_local : inner_local + state_size]
    c_out = convolved[:, inner_local + state_size :]
    step_size = jax.nn.softplus(step_raw + step_bias[None, :])
    log_step = -decay_rate[None, :] * step_size

    xs = values.reshape(block_count, block_rows, head_count, head_dim).transpose(0, 2, 1, 3)
    bs = b_in.reshape(block_count, block_rows, state_size)
    cs = c_out.reshape(block_count, block_rows, state_size)
    logs = log_step.reshape(block_count, block_rows, head_count).transpose(0, 2, 1)
    steps = step_size.reshape(block_count, block_rows, head_count).transpose(0, 2, 1)
    lower = jnp.arange(block_rows)[:, None]
    upper = jnp.arange(block_rows)[None, :]
    summing = ((lower >= upper) if backward else (lower <= upper)).astype(jnp.float32)
    running = jnp.einsum("bhj,ji->bhi", logs, summing, precision=HIGHEST)
    totals = running[:, :, 0] if backward else running[:, :, -1]

    weighting = jnp.exp(totals[:, :, None] - running) * steps
    ends = jnp.einsum("bhj,bhjp,bjn->bhpn", weighting, xs, bs, precision=HIGH)
    order = list(range(block_count))
    if backward:
        order = order[::-1]
    prefix = {order[0]: jnp.zeros_like(ends[0])}
    for before, block in zip(order[:-1], order[1:]):
        prefix[block] = jnp.exp(totals[before])[:, None, None] * prefix[before] + ends[before]
    last = order[-1]
    memory = jnp.exp(totals[last])[:, None, None] * prefix[last] + ends[last]
    prefix = jnp.stack([prefix[block] for block in range(block_count)])
    offsets = lax.cumsum(totals, axis=0, reverse=backward) - totals
    total_log = jnp.sum(totals, axis=0)

    rows = jnp.arange(block_rows)[:, None]
    cols = jnp.arange(block_rows)[None, :]
    causal = ((rows <= cols) if backward else (rows >= cols))[None, None]
    spread = jnp.where(causal, running[:, :, :, None] - running[:, :, None, :], 0.0)
    weights = jnp.where(causal, jnp.exp(spread), 0.0)
    intersection = jnp.einsum("bin,bjn->bij", cs, bs, precision=HIGH)
    mixing = intersection[:, None] * weights * steps[:, :, None, :]
    inside = jnp.einsum("bhij,bhjp->bhip", mixing, xs, precision=HIGH)
    carried = jnp.einsum("bin,bhpn->bhip", cs, prefix, precision=HIGH)
    outputs = inside + carried * jnp.exp(running)[..., None]
    outputs = outputs + skip_gain[None, :, None, None] * xs
    outputs = outputs.transpose(0, 2, 1, 3).reshape(length, inner_local)
    reach = (offsets[:, :, None] + running).transpose(0, 2, 1).reshape(length, head_count)
    gate = jax.nn.silu(gate)
    return dict(outputs=outputs, c_out=c_out, reach=reach, memory=memory, total_log=total_log,
                gate=gate)


def finish_strand(parts, incoming):
    entering = jnp.einsum("tn,hpn->thp", parts["c_out"], incoming, precision=HIGH)
    entering = entering * jnp.exp(parts["reach"])[:, :, None]
    outputs = parts["outputs"] + entering.reshape(parts["outputs"].shape)
    return outputs * parts["gate"]


def relay(total_log, memory, axis, direction):
    count = lax.axis_size(axis)
    head_count, head_dim, state_size = memory.shape
    factor = jnp.broadcast_to(jnp.exp(total_log)[:, None, None], (head_count, 1, state_size))
    own = jnp.concatenate([memory, factor], axis=1)
    near = shifted(own, axis, direction)
    far = shifted(own, axis, 2 * direction)
    state = near[:, :head_dim] + near[:, head_dim:] * far[:, :head_dim]
    packed = jnp.concatenate([state, near[:, head_dim:] * far[:, head_dim:]], axis=1)
    distance = 2
    while distance < count:
        arrived = shifted(packed, axis, direction * distance)
        state = packed[:, :head_dim] + packed[:, head_dim:] * arrived[:, :head_dim]
        factor = packed[:, head_dim:] * arrived[:, head_dim:]
        packed = jnp.concatenate([state, factor], axis=1)
        distance *= 2
    return packed[:, :head_dim]


def local_body(
    nucleotides,
    complement,
    embedding,
    w_gate,
    w_value,
    w_state,
    w_step,
    step_bias,
    decay_rate,
    conv_value,
    conv_state,
    skip_gain,
    norm_weight,
    w_out,
):
    inner_local = w_gate.shape[1]
    state_size = w_state.shape[1] // 2
    head_count = step_bias.shape[0]
    head_dim = inner_local // head_count
    vocab_size = embedding.shape[0]
    table = jnp.concatenate([w_gate, w_value, w_state, w_step], axis=1)
    projected = jnp.dot(embedding, table, precision=HIGH)
    kernel = jnp.concatenate([conv_value, conv_state], axis=1)
    symbols = jnp.arange(vocab_size, dtype=jnp.int32)
    forward_match = nucleotides[:, None] == symbols[None, :]
    paired_ids = jnp.sum(jnp.where(forward_match, complement[None, :], 0), axis=1)
    reverse_hot = (paired_ids[:, None] == symbols[None, :]).astype(jnp.float32)
    forward_hot = forward_match.astype(jnp.float32)
    edge_rows = CONV - 1
    rim_forward_hot = shifted(forward_hot[-edge_rows:], "ctx", 1)
    rim_reverse_hot = shifted(reverse_hot[:edge_rows], "ctx", -1)
    split_step = 2 * inner_local + 2 * state_size
    conv_table = projected[:, inner_local:split_step]
    forward_rows = jnp.dot(forward_hot, projected, precision=HIGHEST)
    reverse_rows = jnp.dot(reverse_hot, projected, precision=HIGHEST)
    rim_forward = jnp.dot(rim_forward_hot, conv_table, precision=HIGHEST)
    rim_reverse = jnp.dot(rim_reverse_hot, conv_table, precision=HIGHEST)
    parts_f = strand_local(forward_rows[:, inner_local:split_step], rim_forward, kernel,
                           forward_rows[:, split_step:], step_bias, decay_rate, skip_gain,
                           forward_rows[:, :inner_local], inner_local, state_size, head_dim, BLK,
                           False)
    parts_r = strand_local(reverse_rows[:, inner_local:split_step], rim_reverse, kernel,
                           reverse_rows[:, split_step:], step_bias, decay_rate, skip_gain,
                           reverse_rows[:, :inner_local], inner_local, state_size, head_dim, BLK,
                           True)
    incoming_f = relay(parts_f["total_log"], parts_f["memory"], "ctx", 1)
    incoming_r = relay(parts_r["total_log"], parts_r["memory"], "ctx", -1)
    gated_f = finish_strand(parts_f, incoming_f)
    gated_r = finish_strand(parts_r, incoming_r)
    square_sums = lax.psum(
        (jnp.sum(gated_f * gated_f, axis=1), jnp.sum(gated_r * gated_r, axis=1)), "tp"
    )
    width_all = inner_local * lax.axis_size("tp")
    normed_f = (
        gated_f * lax.rsqrt(square_sums[0] / width_all + EPSILON)[:, None] * norm_weight[None, :]
    )
    normed_r = (
        gated_r * lax.rsqrt(square_sums[1] / width_all + EPSILON)[:, None] * norm_weight[None, :]
    )
    combined = normed_f + normed_r
    tp_count = lax.axis_size("tp")
    rows_each = combined.shape[0] // tp_count
    own = lax.axis_index("tp")
    result = None
    for turn in range(1, tp_count):
        target = (own + turn) % tp_count
        rows = lax.dynamic_slice_in_dim(combined, target * rows_each, rows_each, 0)
        partial = jnp.dot(rows, w_out, precision=HIGH)
        pairs = [(source, (source + turn) % tp_count) for source in range(tp_count)]
        arrived = lax.ppermute(partial, "tp", pairs)
        result = arrived if result is None else result + arrived
    rows = lax.dynamic_slice_in_dim(combined, own * rows_each, rows_each, 0)
    return jnp.dot(rows, w_out, precision=HIGH) + result


def solution(mesh):
    placed = (
        P(("dp", "ctx")),
        P(),
        P(),
        P(None, "tp"),
        P(None, "tp"),
        P(),
        P(None, "tp"),
        P("tp"),
        P("tp"),
        P(None, "tp"),
        P(),
        P("tp"),
        P("tp"),
        P("tp", None),
    )
    return jax.shard_map(
        local_body, mesh=mesh, in_specs=placed, out_specs=P(("dp", "ctx", "tp"), None), check_vma=False
    )
```

```python
import jax
import jax.numpy as jnp
from jax import lax
from jax.sharding import PartitionSpec as P


CONV = 4
BLK = 256


HIGHEST = lax.Precision.HIGHEST
HIGH = lax.Precision.HIGH
EPSILON = 1e-05


def shifted(value, axis, steps):
    count = lax.axis_size(axis)
    first, last = (max(0, -steps), min(count, count - steps))
    return lax.ppermute(value, axis, [(source, source + steps) for source in range(first, last)])


def causal_conv(padded, kernel):
    length = padded.shape[0] - kernel.shape[0] + 1
    output = jnp.zeros((length, padded.shape[1]), jnp.float32)
    for offset in range(kernel.shape[0]):
        output = output + kernel[offset][None, :] * padded[offset : offset + length]
    return output


def strand_local(joined_in, rim_rows, kernel, step_raw, step_bias, decay_rate, skip_gain,
                 gate, inner_local, state_size, head_dim, block_rows, backward):
    if backward:
        padded = jnp.concatenate([joined_in, rim_rows], axis=0)
        kernel = kernel[::-1]
    else:
        padded = jnp.concatenate([rim_rows, joined_in], axis=0)
    convolved = jax.nn.silu(causal_conv(padded, kernel))
    length = joined_in.shape[0]
    head_count = inner_local // head_dim
    block_count = length // block_rows
    values = convolved[:, :inner_local]
    b_in = convolved[:, inner_local : inner_local + state_size]
    c_out = convolved[:, inner_local + state_size :]
    step_size = jax.nn.softplus(step_raw + step_bias[None, :])
    log_step = -decay_rate[None, :] * step_size

    xs = values.reshape(block_count, block_rows, head_count, head_dim).transpose(0, 2, 1, 3)
    bs = b_in.reshape(block_count, block_rows, state_size)
    cs = c_out.reshape(block_count, block_rows, state_size)
    logs = log_step.reshape(block_count, block_rows, head_count).transpose(0, 2, 1)
    steps = step_size.reshape(block_count, block_rows, head_count).transpose(0, 2, 1)
    lower = jnp.arange(block_rows)[:, None]
    upper = jnp.arange(block_rows)[None, :]
    summing = ((lower >= upper) if backward else (lower <= upper)).astype(jnp.float32)
    running = jnp.einsum("bhj,ji->bhi", logs, summing, precision=HIGHEST)
    totals = running[:, :, 0] if backward else running[:, :, -1]

    weighting = jnp.exp(totals[:, :, None] - running) * steps
    ends = jnp.einsum("bhj,bhjp,bjn->bhpn", weighting, xs, bs, precision=HIGH)
    order = list(range(block_count))
    if backward:
        order = order[::-1]
    prefix = {order[0]: jnp.zeros_like(ends[0])}
    for before, block in zip(order[:-1], order[1:]):
        prefix[block] = jnp.exp(totals[before])[:, None, None] * prefix[before] + ends[before]
    last = order[-1]
    memory = jnp.exp(totals[last])[:, None, None] * prefix[last] + ends[last]
    prefix = jnp.stack([prefix[block] for block in range(block_count)])
    offsets = lax.cumsum(totals, axis=0, reverse=backward) - totals
    total_log = jnp.sum(totals, axis=0)

    rows = jnp.arange(block_rows)[:, None]
    cols = jnp.arange(block_rows)[None, :]
    causal = ((rows <= cols) if backward else (rows >= cols))[None, None]
    spread = jnp.where(causal, running[:, :, :, None] - running[:, :, None, :], 0.0)
    weights = jnp.where(causal, jnp.exp(spread), 0.0)
    intersection = jnp.einsum("bin,bjn->bij", cs, bs, precision=HIGH)
    mixing = intersection[:, None] * weights * steps[:, :, None, :]
    inside = jnp.einsum("bhij,bhjp->bhip", mixing, xs, precision=HIGH)
    carried = jnp.einsum("bin,bhpn->bhip", cs, prefix, precision=HIGH)
    outputs = inside + carried * jnp.exp(running)[..., None]
    outputs = outputs + skip_gain[None, :, None, None] * xs
    outputs = outputs.transpose(0, 2, 1, 3).reshape(length, inner_local)
    reach = (offsets[:, :, None] + running).transpose(0, 2, 1).reshape(length, head_count)
    gate = jax.nn.silu(gate)
    return dict(outputs=outputs, c_out=c_out, reach=reach, memory=memory, total_log=total_log,
                gate=gate)


def finish_strand(parts, incoming):
    entering = jnp.einsum("tn,hpn->thp", parts["c_out"], incoming, precision=HIGH)
    entering = entering * jnp.exp(parts["reach"])[:, :, None]
    outputs = parts["outputs"] + entering.reshape(parts["outputs"].shape)
    return outputs * parts["gate"]


def relay(total_log, memory, axis, direction):
    count = lax.axis_size(axis)
    head_count, head_dim, state_size = memory.shape
    factor = jnp.broadcast_to(jnp.exp(total_log)[:, None, None], (head_count, 1, state_size))
    own = jnp.concatenate([memory, factor], axis=1)
    near = shifted(own, axis, direction)
    far = shifted(own, axis, 2 * direction)
    state = near[:, :head_dim] + near[:, head_dim:] * far[:, :head_dim]
    packed = jnp.concatenate([state, near[:, head_dim:] * far[:, head_dim:]], axis=1)
    distance = 2
    while distance < count:
        arrived = shifted(packed, axis, direction * distance)
        state = packed[:, :head_dim] + packed[:, head_dim:] * arrived[:, :head_dim]
        factor = packed[:, head_dim:] * arrived[:, head_dim:]
        packed = jnp.concatenate([state, factor], axis=1)
        distance *= 2
    return packed[:, :head_dim]


def local_body(
    nucleotides,
    complement,
    embedding,
    w_gate,
    w_value,
    w_state,
    w_step,
    step_bias,
    decay_rate,
    conv_value,
    conv_state,
    skip_gain,
    norm_weight,
    w_out,
):
    inner_local = w_gate.shape[1]
    state_size = w_state.shape[1] // 2
    head_count = step_bias.shape[0]
    head_dim = inner_local // head_count
    vocab_size = embedding.shape[0]
    table = jnp.concatenate([w_gate, w_value, w_state, w_step], axis=1)
    projected = jnp.dot(embedding, table, precision=HIGH)
    kernel = jnp.concatenate([conv_value, conv_state], axis=1)
    symbols = jnp.arange(vocab_size, dtype=jnp.int32)
    forward_match = nucleotides[:, None] == symbols[None, :]
    paired_ids = jnp.sum(jnp.where(forward_match, complement[None, :], 0), axis=1)
    reverse_hot = (paired_ids[:, None] == symbols[None, :]).astype(jnp.float32)
    forward_hot = forward_match.astype(jnp.float32)
    edge_rows = CONV - 1
    rim_forward_hot = shifted(forward_hot[-edge_rows:], "ctx", 1)
    rim_reverse_hot = shifted(reverse_hot[:edge_rows], "ctx", -1)
    split_step = 2 * inner_local + 2 * state_size
    conv_table = projected[:, inner_local:split_step]
    forward_rows = jnp.dot(forward_hot, projected, precision=HIGH)
    reverse_rows = jnp.dot(reverse_hot, projected, precision=HIGH)
    rim_forward = jnp.dot(rim_forward_hot, conv_table, precision=HIGH)
    rim_reverse = jnp.dot(rim_reverse_hot, conv_table, precision=HIGH)
    parts_f = strand_local(forward_rows[:, inner_local:split_step], rim_forward, kernel,
                           forward_rows[:, split_step:], step_bias, decay_rate, skip_gain,
                           forward_rows[:, :inner_local], inner_local, state_size, head_dim, BLK,
                           False)
    parts_r = strand_local(reverse_rows[:, inner_local:split_step], rim_reverse, kernel,
                           reverse_rows[:, split_step:], step_bias, decay_rate, skip_gain,
                           reverse_rows[:, :inner_local], inner_local, state_size, head_dim, BLK,
                           True)
    incoming_f = relay(parts_f["total_log"], parts_f["memory"], "ctx", 1)
    incoming_r = relay(parts_r["total_log"], parts_r["memory"], "ctx", -1)
    gated_f = finish_strand(parts_f, incoming_f)
    gated_r = finish_strand(parts_r, incoming_r)
    square_sums = lax.psum(
        (jnp.sum(gated_f * gated_f, axis=1), jnp.sum(gated_r * gated_r, axis=1)), "tp"
    )
    width_all = inner_local * lax.axis_size("tp")
    normed_f = (
        gated_f * lax.rsqrt(square_sums[0] / width_all + EPSILON)[:, None] * norm_weight[None, :]
    )
    normed_r = (
        gated_r * lax.rsqrt(square_sums[1] / width_all + EPSILON)[:, None] * norm_weight[None, :]
    )
    combined = normed_f + normed_r
    tp_count = lax.axis_size("tp")
    rows_each = combined.shape[0] // tp_count
    own = lax.axis_index("tp")
    result = None
    for turn in range(1, tp_count):
        target = (own + turn) % tp_count
        rows = lax.dynamic_slice_in_dim(combined, target * rows_each, rows_each, 0)
        partial = jnp.dot(rows, w_out, precision=HIGH)
        pairs = [(source, (source + turn) % tp_count) for source in range(tp_count)]
        arrived = lax.ppermute(partial, "tp", pairs)
        result = arrived if result is None else result + arrived
    rows = lax.dynamic_slice_in_dim(combined, own * rows_each, rows_each, 0)
    return jnp.dot(rows, w_out, precision=HIGH) + result


def solution(mesh):
    placed = (
        P(("dp", "ctx")),
        P(),
        P(),
        P(None, "tp"),
        P(None, "tp"),
        P(),
        P(None, "tp"),
        P("tp"),
        P("tp"),
        P(None, "tp"),
        P(),
        P("tp"),
        P("tp"),
        P("tp", None),
    )
    return jax.shard_map(
        local_body, mesh=mesh, in_specs=placed, out_specs=P(("dp", "ctx", "tp"), None), check_vma=False
    )
```

```python
import jax
import jax.numpy as jnp
from jax import lax
from jax.sharding import PartitionSpec as P


CONV = 4
BLK = 256


HIGHEST = lax.Precision.HIGHEST
HIGH = lax.Precision.HIGH
EPSILON = 1e-05


def shifted(value, axis, steps):
    count = lax.axis_size(axis)
    first, last = (max(0, -steps), min(count, count - steps))
    return lax.ppermute(value, axis, [(source, source + steps) for source in range(first, last)])


def causal_conv(padded, kernel):
    length = padded.shape[0] - kernel.shape[0] + 1
    output = jnp.zeros((length, padded.shape[1]), jnp.float32)
    for offset in range(kernel.shape[0]):
        output = output + kernel[offset][None, :] * padded[offset : offset + length]
    return output


def strand_local(joined_in, rim_rows, kernel, step_raw, step_bias, decay_rate, skip_gain,
                 gate, inner_local, state_size, head_dim, block_rows, backward):
    if backward:
        padded = jnp.concatenate([joined_in, rim_rows], axis=0)
        kernel = kernel[::-1]
    else:
        padded = jnp.concatenate([rim_rows, joined_in], axis=0)
    convolved = jax.nn.silu(causal_conv(padded, kernel))
    length = joined_in.shape[0]
    head_count = inner_local // head_dim
    block_count = length // block_rows
    values = convolved[:, :inner_local]
    b_in = convolved[:, inner_local : inner_local + state_size]
    c_out = convolved[:, inner_local + state_size :]
    step_size = jax.nn.softplus(step_raw + step_bias[None, :])
    log_step = -decay_rate[None, :] * step_size

    xs = values.reshape(block_count, block_rows, head_count, head_dim).transpose(0, 2, 1, 3)
    bs = b_in.reshape(block_count, block_rows, state_size)
    cs = c_out.reshape(block_count, block_rows, state_size)
    logs = log_step.reshape(block_count, block_rows, head_count).transpose(0, 2, 1)
    steps = step_size.reshape(block_count, block_rows, head_count).transpose(0, 2, 1)
    lower = jnp.arange(block_rows)[:, None]
    upper = jnp.arange(block_rows)[None, :]
    summing = ((lower >= upper) if backward else (lower <= upper)).astype(jnp.float32)
    running = jnp.einsum("bhj,ji->bhi", logs, summing, precision=HIGHEST)
    totals = running[:, :, 0] if backward else running[:, :, -1]

    weighting = jnp.exp(totals[:, :, None] - running) * steps
    ends = jnp.einsum("bhj,bhjp,bjn->bhpn", weighting, xs, bs, precision=HIGH)
    order = list(range(block_count))
    if backward:
        order = order[::-1]
    prefix = {order[0]: jnp.zeros_like(ends[0])}
    for before, block in zip(order[:-1], order[1:]):
        prefix[block] = jnp.exp(totals[before])[:, None, None] * prefix[before] + ends[before]
    last = order[-1]
    memory = jnp.exp(totals[last])[:, None, None] * prefix[last] + ends[last]
    prefix = jnp.stack([prefix[block] for block in range(block_count)])
    offsets = lax.cumsum(totals, axis=0, reverse=backward) - totals
    total_log = jnp.sum(totals, axis=0)

    rows = jnp.arange(block_rows)[:, None]
    cols = jnp.arange(block_rows)[None, :]
    causal = ((rows <= cols) if backward else (rows >= cols))[None, None]
    spread = jnp.where(causal, running[:, :, :, None] - running[:, :, None, :], 0.0)
    weights = jnp.where(causal, jnp.exp(spread), 0.0)
    intersection = jnp.einsum("bin,bjn->bij", cs, bs, precision=HIGH)
    mixing = intersection[:, None] * weights * steps[:, :, None, :]
    inside = jnp.einsum("bhij,bhjp->bhip", mixing, xs, precision=HIGH)
    carried = jnp.einsum("bin,bhpn->bhip", cs, prefix, precision=HIGH)
    outputs = inside + carried * jnp.exp(running)[..., None]
    outputs = outputs + skip_gain[None, :, None, None] * xs
    outputs = outputs.transpose(0, 2, 1, 3).reshape(length, inner_local)
    reach = (offsets[:, :, None] + running).transpose(0, 2, 1).reshape(length, head_count)
    gate = jax.nn.silu(gate)
    return dict(outputs=outputs, c_out=c_out, reach=reach, memory=memory, total_log=total_log,
                gate=gate)


def finish_strand(parts, incoming):
    entering = jnp.einsum("tn,hpn->thp", parts["c_out"], incoming, precision=HIGH)
    entering = entering * jnp.exp(parts["reach"])[:, :, None]
    outputs = parts["outputs"] + entering.reshape(parts["outputs"].shape)
    return outputs * parts["gate"]


def relay(total_log, memory, axis, direction):
    count = lax.axis_size(axis)
    head_count, head_dim, state_size = memory.shape
    factor = jnp.broadcast_to(jnp.exp(total_log)[:, None, None], (head_count, 1, state_size))
    own = jnp.concatenate([memory, factor], axis=1)
    near = shifted(own, axis, direction)
    far = shifted(own, axis, 2 * direction)
    state = near[:, :head_dim] + near[:, head_dim:] * far[:, :head_dim]
    packed = jnp.concatenate([state, near[:, head_dim:] * far[:, head_dim:]], axis=1)
    distance = 2
    while distance < count:
        arrived = shifted(packed, axis, direction * distance)
        state = packed[:, :head_dim] + packed[:, head_dim:] * arrived[:, :head_dim]
        factor = packed[:, head_dim:] * arrived[:, head_dim:]
        packed = jnp.concatenate([state, factor], axis=1)
        distance *= 2
    return packed[:, :head_dim]


def local_body(
    nucleotides,
    complement,
    embedding,
    w_gate,
    w_value,
    w_state,
    w_step,
    step_bias,
    decay_rate,
    conv_value,
    conv_state,
    skip_gain,
    norm_weight,
    w_out,
):
    inner_local = w_gate.shape[1]
    state_size = w_state.shape[1] // 2
    head_count = step_bias.shape[0]
    head_dim = inner_local // head_count
    vocab_size = embedding.shape[0]
    table = jnp.concatenate([w_value, w_state, w_step], axis=1)
    projected = jnp.dot(embedding, table, precision=HIGH)
    gate_table = jnp.dot(embedding, w_gate, precision=HIGH)
    kernel = jnp.concatenate([conv_value, conv_state], axis=1)
    symbols = jnp.arange(vocab_size, dtype=jnp.int32)
    forward_match = nucleotides[:, None] == symbols[None, :]
    paired_ids = jnp.sum(jnp.where(forward_match, complement[None, :], 0), axis=1)
    reverse_hot = (paired_ids[:, None] == symbols[None, :]).astype(jnp.float32)
    forward_hot = forward_match.astype(jnp.float32)
    edge_rows = CONV - 1
    rim_forward_hot = shifted(forward_hot[-edge_rows:], "ctx", 1)
    rim_reverse_hot = shifted(reverse_hot[:edge_rows], "ctx", -1)
    split_step = inner_local + 2 * state_size
    conv_table = projected[:, :split_step]
    forward_rows = jnp.dot(forward_hot, projected, precision=HIGH)
    reverse_rows = jnp.dot(reverse_hot, projected, precision=HIGH)
    rim_forward = jnp.dot(rim_forward_hot, conv_table, precision=HIGH)
    rim_reverse = jnp.dot(rim_reverse_hot, conv_table, precision=HIGH)
    parts_f = strand_local(forward_rows[:, :split_step], rim_forward, kernel,
                           forward_rows[:, split_step:], step_bias, decay_rate, skip_gain,
                           jnp.dot(forward_hot, gate_table, precision=HIGH), inner_local, state_size, head_dim, BLK,
                           False)
    parts_r = strand_local(reverse_rows[:, :split_step], rim_reverse, kernel,
                           reverse_rows[:, split_step:], step_bias, decay_rate, skip_gain,
                           jnp.dot(reverse_hot, gate_table, precision=HIGH), inner_local, state_size, head_dim, BLK,
                           True)
    incoming_f = relay(parts_f["total_log"], parts_f["memory"], "ctx", 1)
    incoming_r = relay(parts_r["total_log"], parts_r["memory"], "ctx", -1)
    gated_f = finish_strand(parts_f, incoming_f)
    gated_r = finish_strand(parts_r, incoming_r)
    square_sums = lax.psum(
        (jnp.sum(gated_f * gated_f, axis=1), jnp.sum(gated_r * gated_r, axis=1)), "tp"
    )
    width_all = inner_local * lax.axis_size("tp")
    normed_f = (
        gated_f * lax.rsqrt(square_sums[0] / width_all + EPSILON)[:, None] * norm_weight[None, :]
    )
    normed_r = (
        gated_r * lax.rsqrt(square_sums[1] / width_all + EPSILON)[:, None] * norm_weight[None, :]
    )
    combined = normed_f + normed_r
    tp_count = lax.axis_size("tp")
    rows_each = combined.shape[0] // tp_count
    own = lax.axis_index("tp")
    result = None
    for turn in range(1, tp_count):
        target = (own + turn) % tp_count
        rows = lax.dynamic_slice_in_dim(combined, target * rows_each, rows_each, 0)
        partial = jnp.dot(rows, w_out, precision=HIGH)
        pairs = [(source, (source + turn) % tp_count) for source in range(tp_count)]
        arrived = lax.ppermute(partial, "tp", pairs)
        result = arrived if result is None else result + arrived
    rows = lax.dynamic_slice_in_dim(combined, own * rows_each, rows_each, 0)
    return jnp.dot(rows, w_out, precision=HIGH) + result


def solution(mesh):
    placed = (
        P(("dp", "ctx")),
        P(),
        P(),
        P(None, "tp"),
        P(None, "tp"),
        P(),
        P(None, "tp"),
        P("tp"),
        P("tp"),
        P(None, "tp"),
        P(),
        P("tp"),
        P("tp"),
        P("tp", None),
    )
    return jax.shard_map(
        local_body, mesh=mesh, in_specs=placed, out_specs=P(("dp", "ctx", "tp"), None), check_vma=False
    )
```
